128 devices in a mesh: grp: 4 (over z), seq: 32 (over x, y, core).
Axes of the slice: x: 4, y: 4, z: 4, core: 2. Of those that a mesh axis runs over, the one named last changes fastest.
Arguments:
- tokens: bfloat16 [131072, 512], P(('grp', 'seq')), may hold values from -6 to 6
- norm_gain1: float32 [512], replicated, may hold values from 0.5 to 1.5
- w_xz: bfloat16 [512, 2048], replicated, may hold values from -0.25 to 0.25
- w_bc: bfloat16 [512, 256], replicated, may hold values from -0.0234375 to 0.0234375
- w_dt: bfloat16 [512, 16], replicated, may hold values from -0.25 to 0.25
- dt_bias: float32 [16], replicated, may hold values from -1 to 1
- decay_rate: float32 [16], replicated, may hold values from 3.8146973e-07 to 0.08
- curve_jump: float32 [131072], P(('grp', 'seq')), may hold values from 0 to 1.4
- skip_gain: float32 [16], replicated, may hold values from 0.3 to 1
- norm_gain2: float32 [1024], replicated, may hold values from 0.5 to 1.5
- w_out: bfloat16 [1024, 512], replicated, may hold values from -0.1875 to 0.1875
- norm_gain3: float32 [512], replicated, may hold values from 0.5 to 1.5
- w_q: bfloat16 [512, 1024], replicated, may hold values from -15.909903 to 15.909903
- w_kv: bfloat16 [512, 2048], replicated, may hold values from -0.25 to 0.25
- w_o: bfloat16 [1024, 512], replicated, may hold values from -0.1875 to 0.1875
- nbr_owner: int32 [2048, 2], P(('grp', 'seq')), may hold values from 0 to 31, all different within a row; in each aligned block of 16 rows (0 to 15, 16 to 31, ...) at most 2 rows name the same one
- nbr_block: int32 [2048, 2], P(('grp', 'seq')), may hold values from 0 to 15
Outputs:
- layer_out: bfloat16 [131072, 512], P(('grp', 'seq'))
The draws below stay inside these ranges and needn't reach their ends.
Inputs may be any that keep to these rules, and one draw needn't show every extreme that they name: `nbr_owner`: no two slots of one block name the same owner; among the lists of one device's 16 blocks no owner is named more than 2 times, and in every draw some device names one owner exactly 2 times.
All inputs are finite; a program needn't handle non-finite values.
Results may differ from the reference program's by a relative error of at most 0.023.
Values may be sent and summed in bfloat16 or wider, within the bound.
No kernel may reach another device: no remote copies, remote signals or barrier semaphores. Data moves between devices by JAX's collectives and lax.ppermute only.
A program may use at most 192 MiB of HBM per device.

```python
import math
import jax
import jax.numpy as jnp
import numpy as np
from jax import lax

D = 512
H = 16
P_SIZE = 64
NS = 128
INNER = 1024
CH = 128
BL = 64
KN = 2
TOK_DEV = 1024
BLK_DEV = 16
CAP = 2
TOKENS = 131072
NBLK = 2048
N_GRP = 4
N_SEQ = 32


def draw_decay_rate(key, part):
    first, second, third = jax.random.split(key, 3)
    slow_heads = jax.random.randint(first, (H,), 0, 2) > 0
    slow_rate = jnp.exp(jax.random.uniform(second, (H,), jnp.float32, math.log(0.05), math.log(0.4))) / TOKENS
    fast_rate = jnp.exp(jax.random.uniform(third, (H,), jnp.float32, math.log(0.03), math.log(0.08)))
    return jnp.where(slow_heads, slow_rate, fast_rate).astype(jnp.float32)


def draw_curve_jump(key, part):
    first, second, third, fourth = jax.random.split(key, 4)
    device_count = TOKENS // TOK_DEV
    device_level = jnp.exp(jax.random.uniform(first, (device_count,), jnp.float32, math.log(0.1), 0.0))
    token_level = jnp.exp(jax.random.uniform(second, (TOKENS,), jnp.float32, math.log(0.5), math.log(2.0)))
    baseline = jnp.repeat(device_level, TOK_DEV) * token_level / TOKENS
    places = jax.random.randint(third, (6,), 0, TOKENS)
    amounts = jax.random.uniform(fourth, (6,), jnp.float32, 0.22, 0.69)
    return baseline.at[places].add(amounts).astype(jnp.float32)


def draw_w_q(key, part):
    first = jax.random.fold_in(key, 0)
    baseline = jnp.clip(jax.random.normal(first, (D, H * P_SIZE), jnp.float32), -6.0, 6.0) / math.sqrt(D)
    return baseline.astype(jnp.bfloat16)


def plant(values, rng, smallest, largest):
    spot = [jax.random.randint(jax.random.fold_in(rng, axis), (), 0, length) for axis, length in enumerate(values.shape)]
    main_axis = values.shape.index(max(values.shape))
    neighbour = spot[:main_axis] + [(spot[main_axis] + 1) % values.shape[main_axis]] + spot[main_axis + 1:]
    return values.at[tuple(spot)].set(smallest).at[tuple(neighbour)].set(largest)


def level_of(stream_key, extent, shards, smallest, top_value):
    level, own = 1.0, jax.random.fold_in(stream_key, 6)
    for dim, parts in shards:
        draws = jnp.exp(jax.random.uniform(jax.random.fold_in(own, dim), (parts,), jnp.float32, smallest / len(shards), top_value / len(shards)))
        level = level * jnp.repeat(draws, extent[dim] // parts).reshape([-1 if axis == dim else 1 for axis in range(len(extent))])
    return level


def shared_out(key, own, number, rows, amount, top, reach, lean):
    sequence = jax.random.permutation(key, amount)
    packed, common = load_shares(amount, rows * top, reach, lean, True), load_shares(amount, rows * top, reach, lean, False)
    places = jnp.arange(amount)

    def named(sizes, turn):
        used = int((sizes > 0).sum())
        fixed = max(1, used // 4)
        shifted = fixed + (places - fixed + turn * (used - fixed)) % max(1, amount - fixed)
        return jnp.zeros((amount,), jnp.int32).at[sequence[jnp.where(places < fixed, places, shifted)]].set(jnp.asarray(sizes, jnp.int32))

    sizes = jnp.where(number % 4 == 0, named(packed, number // 4), named(common, number - number // 4 - 1))
    mixed = jax.random.permutation(jax.random.fold_in(own, 3), amount)
    donor, sink = mixed[0:amount // 2 * 2:2], mixed[1:amount // 2 * 2:2]
    margin = jnp.minimum(sizes[donor] - 1, reach - sizes[sink]) // 2
    margin = jnp.where((donor == sequence[0]) | (sink == sequence[0]) | (sizes[sink] == 0), 0, jnp.maximum(margin, 0))
    shifted = jax.random.randint(jax.random.fold_in(own, 4), (amount // 2,), 0, 1 << 20) % (margin + 1)
    sizes = sizes.at[donor].add(-shifted).at[sink].add(shifted)
    labels = jnp.searchsorted(jnp.cumsum(sizes), jnp.arange(rows * top), side="right").astype(jnp.int32)
    grid = labels.reshape(top, rows).T
    grid = grid[jax.random.permutation(jax.random.fold_in(own, 1), rows)]
    turn = jax.random.randint(jax.random.fold_in(own, 2), (rows, 1), 0, top)
    return jnp.take_along_axis(grid, (jnp.arange(top)[None, :] + turn) % top, axis=1)


def load_shares(number_of, total, bound, skew, full):
    weights = [(1 << 20) // math.isqrt(grade ** skew) + 1 for grade in range(1, number_of + 1)]
    largest = bound if full else min(bound, max(-(-total // number_of), total * weights[0] // sum(weights)))
    least = 1 if total - largest >= number_of - 1 else 0
    given, surplus = [largest] + [least] * (number_of - 1), total - largest - least * (number_of - 1)
    while surplus > 0:
        movable = [i for i in range(1, number_of) if given[i] < largest] or [i for i in range(1, number_of) if given[i] < bound]
        pool, left = sum([weights[i] for i in movable]), surplus
        for i in movable:
            more = min(bound - given[i], max(1, left * weights[i] // pool), surplus)
            given[i] = given[i] + more
            surplus = surplus - more
    return np.array(given)


def noise(rng, shape, scale, reach, shards=(), held_as=jnp.bfloat16):
    array = jax.random.normal(rng, shape, jnp.float32) * scale
    if len(shards) > 0:
        array = level_of(rng, shape, shards, -0.22, 0.18) * array
    return jnp.clip(array, min=-reach, max=reach).astype(held_as)


def setup_inputs(seed: int = 0) -> dict:
    seeds = jax.random.split(jax.random.key(seed), 18)
    tokens = noise(seeds[0], (TOKENS, D), 1.0, 6.0, ((0, 128),))
    norm_gain1 = jnp.clip(jax.random.uniform(seeds[1], (D,), jnp.float32, 0.5, 1.5), 0.5, 1.5)
    w_xz = noise(seeds[2], (D, 2 * INNER), D ** -0.5, 0.25)
    w_bc = noise(seeds[3], (D, 2 * NS), (D * NS) ** -0.5, 0.0234375)
    w_dt = noise(seeds[4], (D, H), D ** -0.5, 0.25)
    dt_bias = jnp.clip(jax.random.uniform(seeds[5], (H,), jnp.float32, -1.0, 1.0), -1.0, 1.0)
    decay_rate = draw_decay_rate(jax.random.fold_in(seeds[17], 71), 0)
    curve_jump = draw_curve_jump(jax.random.fold_in(seeds[17], 71), 0)
    skip_gain = jnp.clip(jax.random.uniform(seeds[8], (H,), jnp.float32, 0.3, 1.0), 0.3, 1.0)
    norm_gain2 = jnp.clip(jax.random.uniform(seeds[9], (INNER,), jnp.float32, 0.5, 1.5), 0.5, 1.5)
    w_out = noise(seeds[10], (INNER, D), INNER ** -0.5, 0.1875)
    norm_gain3 = jnp.clip(jax.random.uniform(seeds[11], (D,), jnp.float32, 0.5, 1.5), 0.5, 1.5)
    w_q = draw_w_q(jax.random.fold_in(seeds[17], 71), 0)
    w_kv = noise(seeds[13], (D, 2 * INNER), D ** -0.5, 0.25)
    w_o = noise(seeds[14], (INNER, D), INNER ** -0.5, 0.1875)
    nbr_owner_keys = jax.random.split(jax.random.fold_in(seeds[15], 1), NBLK // BLK_DEV)
    nbr_owner_turns = jax.random.permutation(jax.random.fold_in(seeds[15], 3), NBLK // BLK_DEV)
    nbr_owner = jax.vmap(lambda own, number: shared_out(jax.random.fold_in(seeds[15], 2), own, number, BLK_DEV, N_SEQ, KN, CAP, 2))(nbr_owner_keys, nbr_owner_turns).reshape((NBLK, KN))
    nbr_block = plant(jax.random.randint(seeds[16], (NBLK, KN), 0, BLK_DEV), jax.random.fold_in(seeds[16], 1), 0, BLK_DEV - 1).astype(jnp.int32)
    return dict(tokens=tokens, norm_gain1=norm_gain1, w_xz=w_xz, w_bc=w_bc, w_dt=w_dt, dt_bias=dt_bias, decay_rate=decay_rate, curve_jump=curve_jump, skip_gain=skip_gain, norm_gain2=norm_gain2, w_out=w_out, norm_gain3=norm_gain3, w_q=w_q, w_kv=w_kv, w_o=w_o, nbr_owner=nbr_owner, nbr_block=nbr_block)


epsilon = 1e-05
highest = lax.Precision.HIGHEST

def rms_rows(values, weights):
    floats = values.astype(jnp.float32)
    return (floats * lax.rsqrt(lax.optimization_barrier(jnp.mean(floats * floats, axis=-1, keepdims=True)) + epsilon) * weights).astype(jnp.bfloat16)

def mamba_inputs(rows_in, norm_gain1, w_xz, w_bc, w_dt, dt_bias, decay_rate, jump_rows):
    normed = rms_rows(rows_in, norm_gain1)
    stream_gate = jnp.dot(normed, w_xz, preferred_element_type=jnp.float32).astype(jnp.bfloat16)
    maps = jnp.dot(normed, w_bc, preferred_element_type=jnp.float32).astype(jnp.bfloat16)
    step_size = jax.nn.softplus(jnp.dot(normed, w_dt, preferred_element_type=jnp.float32) + dt_bias)
    log_decay = -(decay_rate * step_size + jump_rows[:, None])
    return (stream_gate[:, :INNER], stream_gate[:, INNER:], maps[:, :NS], maps[:, NS:], step_size, log_decay)

def rounded_floats(values):
    return lax.optimization_barrier(values.astype(jnp.bfloat16)).astype(jnp.float32)

def state_scan(stream, input_map, output_map, step_size, log_decay, initial):
    count = stream.shape[0] // CH
    streams = stream.reshape(count, CH, H, P_SIZE)
    inputs = input_map.reshape(count, CH, NS)
    outputs = output_map.reshape(count, CH, NS)
    steps = step_size.reshape(count, CH, H)
    decays = log_decay.reshape(count, CH, H)
    lower = (jnp.arange(CH)[:, None] >= jnp.arange(CH)[None, :])[None]

    def advance(carried, pieces):
        block_x, block_b, block_c, block_u, block_l = pieces
        x_floats = block_x.astype(jnp.float32)
        running = jnp.cumsum(block_l, axis=0)
        across = running.T
        spread = across[:, :, None] - across[:, None, :]
        weights = jnp.where(lower, jnp.exp(jnp.where(lower, spread, 0.0)), 0.0)
        intersection = jnp.dot(block_c, block_b.T, preferred_element_type=jnp.float32)
        mixing = rounded_floats(intersection[None] * weights * block_u.T[:, None, :])
        result = jnp.einsum('hts,shp->thp', mixing, x_floats)
        result = result + jnp.exp(running)[:, :, None] * jnp.einsum('tn,hpn->thp', block_c.astype(jnp.float32), carried, precision=highest)
        tail_weight = jnp.exp(running[-1][None, :] - running) * block_u
        tail = rounded_floats(tail_weight[:, :, None] * x_floats)
        updated = jnp.exp(running[-1])[:, None, None] * carried + jnp.einsum('shp,sn->hpn', tail, block_b.astype(jnp.float32))
        return (updated, result)
    final, results = lax.scan(advance, initial, (streams, inputs, outputs, steps, decays))
    return (results.reshape(count * CH, H, P_SIZE), final)

def mamba_finish(rows_in, mixed_state, stream, gate_in, skip_gain, norm_gain2, w_out):
    total = mixed_state + skip_gain[None, :, None] * stream.astype(jnp.float32).reshape(-1, H, P_SIZE)
    gated = total * jax.nn.silu(gate_in.astype(jnp.float32)).reshape(-1, H, P_SIZE)
    normed = gated * lax.rsqrt(lax.optimization_barrier(jnp.mean(gated * gated, axis=-1, keepdims=True)) + epsilon)
    scaled = (normed.reshape(-1, INNER) * norm_gain2).astype(jnp.bfloat16)
    return (rows_in.astype(jnp.float32) + jnp.dot(scaled, w_out, preferred_element_type=jnp.float32)).astype(jnp.bfloat16)

def attend_blocks(queries, own_keys, own_values, far_keys, far_values):
    score_scale = 1.0 / math.sqrt(P_SIZE)
    query_floats = queries.astype(jnp.float32)
    own_scores = jnp.einsum('bqhd,bkhd->bhqk', query_floats, own_keys.astype(jnp.float32)) * score_scale
    far_scores = jnp.einsum('bqhd,bkhd->bhqk', query_floats, far_keys.astype(jnp.float32)) * score_scale
    peak = jnp.maximum(lax.optimization_barrier(jnp.max(own_scores, axis=-1, keepdims=True)), lax.optimization_barrier(jnp.max(far_scores, axis=-1, keepdims=True)))
    own_exp = jnp.exp(own_scores - peak)
    far_exp = jnp.exp(far_scores - peak)
    denominator = lax.optimization_barrier(jnp.sum(own_exp, axis=-1, keepdims=True)) + lax.optimization_barrier(jnp.sum(far_exp, axis=-1, keepdims=True))
    own_weight = (own_exp / denominator).astype(jnp.bfloat16)
    far_weight = (far_exp / denominator).astype(jnp.bfloat16)
    mixed = jnp.einsum('bhqk,bkhd->bqhd', own_weight.astype(jnp.float32), own_values.astype(jnp.float32))
    mixed = mixed + jnp.einsum('bhqk,bkhd->bqhd', far_weight.astype(jnp.float32), far_values.astype(jnp.float32))
    return mixed.astype(jnp.bfloat16)

def reference(tokens, norm_gain1, w_xz, w_bc, w_dt, dt_bias, decay_rate, curve_jump, skip_gain, norm_gain2, w_out, norm_gain3, w_q, w_kv, w_o, nbr_owner, nbr_block):
    devices = N_GRP * N_SEQ
    token_rows = tokens.reshape(devices, TOK_DEV, D)
    jump_rows = curve_jump.reshape(devices, TOK_DEV)

    def one_device(carried, pieces):
        rows_in, jumps = pieces
        stream, gate_in, input_map, output_map, step_size, log_decay = mamba_inputs(rows_in, norm_gain1, w_xz, w_bc, w_dt, dt_bias, decay_rate, jumps)
        mixed_state, updated = state_scan(stream, input_map, output_map, step_size, log_decay, carried)
        return (updated, mamba_finish(rows_in, mixed_state, stream, gate_in, skip_gain, norm_gain2, w_out))
    start = jnp.zeros((H, P_SIZE, NS), jnp.float32)
    _, middle = lax.scan(one_device, start, (token_rows, jump_rows))
    normed_all = lax.map(lambda rows: rms_rows(rows, norm_gain3), middle)
    key_value = lax.map(lambda rows: jnp.dot(rows, w_kv, preferred_element_type=jnp.float32).astype(jnp.bfloat16), normed_all)
    key_value = key_value.reshape(devices * BLK_DEV, BL, 2 * INNER)

    def attend_device(index):
        normed = normed_all[index]
        queries = jnp.dot(normed, w_q, preferred_element_type=jnp.float32).astype(jnp.bfloat16).reshape(BLK_DEV, BL, H, P_SIZE)
        first = (index * BLK_DEV).astype(jnp.int32)
        own = lax.dynamic_slice_in_dim(key_value, first, BLK_DEV, 0)
        owners = lax.dynamic_slice_in_dim(nbr_owner, first, BLK_DEV, 0)
        blocks = lax.dynamic_slice_in_dim(nbr_block, first, BLK_DEV, 0)
        global_ids = ((index // N_SEQ * N_SEQ + owners) * BLK_DEV + blocks).astype(jnp.int32)
        far = key_value[global_ids.reshape(-1)].reshape(BLK_DEV, KN * BL, 2 * INNER)
        attended = attend_blocks(queries, own[..., :INNER].reshape(BLK_DEV, BL, H, P_SIZE), own[..., INNER:].reshape(BLK_DEV, BL, H, P_SIZE), far[..., :INNER].reshape(BLK_DEV, KN * BL, H, P_SIZE), far[..., INNER:].reshape(BLK_DEV, KN * BL, H, P_SIZE)).reshape(TOK_DEV, INNER)
        return (middle[index].astype(jnp.float32) + jnp.dot(attended, w_o, preferred_element_type=jnp.float32)).astype(jnp.bfloat16)
    result = lax.map(attend_device, jnp.arange(devices, dtype=jnp.int32))
    return result.reshape(TOKENS, D)
```

```python
import math

import jax
import jax.numpy as jnp
from jax import lax
from jax.sharding import PartitionSpec as P

H = 16
P_SIZE = 64
NS = 128
INNER = 1024
CH = 128
BL = 64
KN = 2


epsilon = 1e-05
highest = lax.Precision.HIGHEST
f32 = jnp.float32
bf16 = jnp.bfloat16


def rms_rows(values, weights):
    floats = values.astype(f32)
    return (
        floats * lax.rsqrt(jnp.mean(floats * floats, axis=-1, keepdims=True) + epsilon) * weights
    ).astype(bf16)


def mamba_inputs(rows_in, norm_gain1, w_xz, w_bc, w_dt, dt_bias, decay_rate, jump_rows):
    normed = rms_rows(rows_in, norm_gain1)
    stream_gate = jnp.dot(normed, w_xz, preferred_element_type=f32).astype(bf16)
    maps = jnp.dot(normed, w_bc, preferred_element_type=f32).astype(bf16)
    step_size = jax.nn.softplus(jnp.dot(normed, w_dt, preferred_element_type=f32) + dt_bias)
    log_decay = -(decay_rate * step_size + jump_rows[:, None])
    return (
        stream_gate[:, :INNER],
        stream_gate[:, INNER:],
        maps[:, :NS],
        maps[:, NS:],
        step_size,
        log_decay,
    )


def chunk_parts(stream, input_map, output_map, step_size, log_decay):
    count = stream.shape[0] // CH
    x = stream.reshape(count, CH, H, P_SIZE)
    b = input_map.reshape(count, CH, NS)
    c = output_map.reshape(count, CH, NS)
    u = step_size.reshape(count, CH, H)
    running = jnp.cumsum(log_decay.reshape(count, CH, H), axis=1)
    across = jnp.transpose(running, (0, 2, 1))
    lower = (jnp.arange(CH)[:, None] >= jnp.arange(CH)[None, :])[None, None]
    spread = across[:, :, :, None] - across[:, :, None, :]
    weights = jnp.where(lower, jnp.exp(jnp.where(lower, spread, 0.0)), 0.0)
    intersection = jnp.einsum("ctn,csn->cts", c, b, preferred_element_type=f32)
    u_across = jnp.transpose(u, (0, 2, 1))
    mixing = (intersection[:, None] * weights * u_across[:, :, None, :]).astype(bf16)
    y_intra = jnp.einsum("chts,cshp->cthp", mixing, x, preferred_element_type=f32)
    last = running[:, -1, :]
    tail_weight = jnp.exp(last[:, None, :] - running) * u
    tail = (tail_weight[..., None] * x.astype(f32)).astype(bf16)
    chunk_state = jnp.einsum("cshp,csn->chpn", tail, b, preferred_element_type=f32)
    prefix = [jnp.zeros((H, P_SIZE, NS), f32)]
    before = [jnp.zeros((H,), f32)]
    for k in range(count):
        prefix.append(jnp.exp(last[k])[:, None, None] * prefix[-1] + chunk_state[k])
        before.append(before[-1] + last[k])
    return (
        y_intra,
        jnp.stack(prefix[:count]),
        jnp.stack(before[:count]),
        prefix[count],
        before[count],
        running,
        c,
    )


def device_prefix(total, state, axes, count):
    incl = (total, state)
    excl = (jnp.zeros_like(total), jnp.zeros_like(state))
    shift = 1
    while shift < count:
        perm = [(i, i + shift) for i in range(count - shift)]
        got_total, got_state = lax.ppermute(incl, axes, perm)
        excl = (got_total + excl[0], jnp.exp(excl[0])[:, None, None] * got_state + excl[1])
        if shift * 2 < count:
            incl = (got_total + incl[0], jnp.exp(incl[0])[:, None, None] * got_state + incl[1])
        shift *= 2
    return excl[1]


def mamba_finish(rows_in, mixed_state, stream, gate_in, skip_gain, norm_gain2, w_out):
    total = mixed_state + skip_gain[None, :, None] * stream.astype(f32).reshape(-1, H, P_SIZE)
    gated = total * jax.nn.silu(gate_in.astype(f32)).reshape(-1, H, P_SIZE)
    normed = gated * lax.rsqrt(jnp.mean(gated * gated, axis=-1, keepdims=True) + epsilon)
    scaled = (normed.reshape(-1, INNER) * norm_gain2).astype(bf16)
    return (rows_in.astype(f32) + jnp.dot(scaled, w_out, preferred_element_type=f32)).astype(bf16)


def attend_blocks(queries, own_keys, own_values, far_keys, far_values):
    score_scale = 1.0 / math.sqrt(P_SIZE)
    own_scores = (
        jnp.einsum("bqhd,bkhd->bhqk", queries, own_keys, preferred_element_type=f32) * score_scale
    )
    far_scores = (
        jnp.einsum("bqhd,bkhd->bhqk", queries, far_keys, preferred_element_type=f32) * score_scale
    )
    peak = jnp.maximum(
        jnp.max(own_scores, axis=-1, keepdims=True), jnp.max(far_scores, axis=-1, keepdims=True)
    )
    own_exp = jnp.exp(own_scores - peak)
    far_exp = jnp.exp(far_scores - peak)
    denominator = jnp.sum(own_exp, axis=-1, keepdims=True) + jnp.sum(
        far_exp, axis=-1, keepdims=True
    )
    own_weight = (own_exp / denominator).astype(bf16)
    far_weight = (far_exp / denominator).astype(bf16)
    mixed = jnp.einsum("bhqk,bkhd->bqhd", own_weight, own_values, preferred_element_type=f32)
    mixed = mixed + jnp.einsum(
        "bhqk,bkhd->bqhd", far_weight, far_values, preferred_element_type=f32
    )
    return mixed.astype(bf16)


def slot_ranks(owner_row, seq_count):
    owners_axis = jnp.arange(seq_count, dtype=jnp.int32)
    hits = (owner_row[:, None] == owners_axis[None, :]).astype(jnp.int32)
    return jnp.sum((jnp.cumsum(hits, axis=0) - hits) * hits, axis=1)


def per_device(
    tokens,
    norm_gain1,
    w_xz,
    w_bc,
    w_dt,
    dt_bias,
    decay_rate,
    curve_jump,
    skip_gain,
    norm_gain2,
    w_out,
    norm_gain3,
    w_q,
    w_kv,
    w_o,
    nbr_owner,
    nbr_block,
):
    token_count = tokens.shape[0]
    seq_count = lax.axis_size("seq")
    device_count = lax.axis_size("grp") * seq_count
    block_count = token_count // BL
    request_count = block_count * KN
    slot_count = max(2, -(-request_count // seq_count))

    owner_flat = nbr_owner.reshape(-1)
    block_flat = nbr_block.reshape(-1)
    own_rank = slot_ranks(owner_flat, seq_count)
    owners_all = lax.all_gather(owner_flat, "seq")
    blocks_all = lax.all_gather(block_flat, "seq")
    ranks_all = lax.all_gather(own_rank, "seq")
    me = lax.axis_index("seq")
    slots = jnp.arange(slot_count, dtype=jnp.int32)
    match = (owners_all[:, None, :] == me) & (ranks_all[:, None, :] == slots[None, :, None])
    send_index = jnp.sum(jnp.where(match, blocks_all[:, None, :], 0), axis=2)
    arrival_index = owner_flat * slot_count + own_rank

    stream, gate_in, input_map, output_map, step_size, log_decay = mamba_inputs(
        tokens, norm_gain1, w_xz, w_bc, w_dt, dt_bias, decay_rate, curve_jump
    )
    y_intra, prefix, before, local_state, local_total, running, c = chunk_parts(
        stream, input_map, output_map, step_size, log_decay
    )
    entering = device_prefix(local_total, local_state, ("grp", "seq"), device_count)
    chunk_in = jnp.exp(before)[:, :, None, None] * entering[None] + prefix
    arriving = jnp.einsum("ctn,chpn->cthp", c.astype(f32), chunk_in, precision=highest)
    mixed_state = y_intra + jnp.exp(running)[..., None] * arriving
    mixed_state = mixed_state.reshape(token_count, H, P_SIZE)
    middle = mamba_finish(tokens, mixed_state, stream, gate_in, skip_gain, norm_gain2, w_out)

    normed = rms_rows(middle, norm_gain3)
    queries = jnp.dot(normed, w_q, preferred_element_type=f32).astype(bf16)
    key_value = jnp.dot(normed, w_kv, preferred_element_type=f32).astype(bf16)
    own_rows = normed.reshape(block_count, BL, normed.shape[-1])
    outgoing = own_rows[send_index]
    arrived = lax.all_to_all(outgoing, "seq", split_axis=0, concat_axis=0, tiled=True)
    far_rows = arrived.reshape(seq_count * slot_count, BL, normed.shape[-1])[arrival_index]
    far_kv = jnp.dot(
        far_rows.reshape(request_count * BL, normed.shape[-1]), w_kv, preferred_element_type=f32
    ).astype(bf16)
    far_blocks = far_kv.reshape(block_count, KN * BL, 2 * INNER)
    own_blocks = key_value.reshape(block_count, BL, 2 * INNER)
    attended = attend_blocks(
        queries.reshape(block_count, BL, H, P_SIZE),
        own_blocks[..., :INNER].reshape(block_count, BL, H, P_SIZE),
        own_blocks[..., INNER:].reshape(block_count, BL, H, P_SIZE),
        far_blocks[..., :INNER].reshape(block_count, KN * BL, H, P_SIZE),
        far_blocks[..., INNER:].reshape(block_count, KN * BL, H, P_SIZE),
    ).reshape(token_count, INNER)
    return (
        middle.astype(f32) + jnp.dot(attended, w_o, preferred_element_type=f32)
    ).astype(bf16)


def solution(mesh):
    in_specs = (
        P(("grp", "seq"), None),
        P(),
        P(),
        P(),
        P(),
        P(),
        P(),
        P(("grp", "seq")),
        P(),
        P(),
        P(),
        P(),
        P(),
        P(),
        P(),
        P(("grp", "seq"), None),
        P(("grp", "seq"), None),
    )
    out_specs = P(("grp", "seq"), None)
    return jax.shard_map(
        per_device, mesh=mesh, in_specs=in_specs, out_specs=out_specs, check_vma=False
    )
```

```python
import math

import jax
import jax.numpy as jnp
from jax import lax
from jax.sharding import PartitionSpec as P

H = 16
P_SIZE = 64
NS = 128
INNER = 1024
CH = 128
BL = 64
KN = 2


epsilon = 1e-05
highest = lax.Precision.HIGHEST
f32 = jnp.float32
bf16 = jnp.bfloat16
def rms_rows(values, weights):
    floats = values.astype(f32)
    return (
        floats * lax.rsqrt(jnp.mean(floats * floats, axis=-1, keepdims=True) + epsilon) * weights
    ).astype(bf16)


def heads_of(rows, weight):
    split = weight.reshape(weight.shape[0], H, P_SIZE)
    return jnp.einsum("td,dhe->hte", rows, split, preferred_element_type=f32).astype(bf16)


def chunk_parts(x, b, c, u, log_decay):
    count = x.shape[1] // CH
    xc = x.reshape(H, count, CH, P_SIZE)
    bc = b.reshape(count, CH, NS)
    cc = c.reshape(count, CH, NS)
    uc = u.reshape(H, count, CH)
    running = jnp.cumsum(log_decay.reshape(H, count, CH), axis=2)
    lower = (jnp.arange(CH)[:, None] >= jnp.arange(CH)[None, :])[None, None]
    spread = running[..., :, None] - running[..., None, :]
    weights = jnp.where(lower, jnp.exp(jnp.where(lower, spread, 0.0)), 0.0)
    intersection = jnp.einsum("ctn,csn->cts", cc, bc, preferred_element_type=f32)
    mixing = (intersection[None] * weights * uc[:, :, None, :]).astype(bf16)
    y_intra = jnp.einsum("hcts,hcsp->hctp", mixing, xc, preferred_element_type=f32)
    last = running[..., -1]
    tail_weight = jnp.exp(last[..., None] - running) * uc
    tail = (tail_weight[..., None] * xc.astype(f32)).astype(bf16)
    chunk_state = jnp.einsum("hcsp,csn->hcpn", tail, bc, preferred_element_type=f32)
    prefix = [jnp.zeros((H, P_SIZE, NS), f32)]
    before = [jnp.zeros((H,), f32)]
    for k in range(count):
        prefix.append(jnp.exp(last[:, k])[:, None, None] * prefix[-1] + chunk_state[:, k])
        before.append(before[-1] + last[:, k])
    return (
        y_intra,
        jnp.stack(prefix[:count], axis=1),
        jnp.stack(before[:count], axis=1),
        prefix[count],
        before[count],
        running,
        cc,
    )


def pack_state(total, state):
    extra = jnp.zeros((8, NS), f32).at[0, :H].set(total)
    return jnp.concatenate([state.reshape(H * P_SIZE, NS), extra], axis=0)


def unpack_state(packed):
    return packed[H * P_SIZE, :H], packed[: H * P_SIZE].reshape(H, P_SIZE, NS)


def device_prefix(total, state, axes, count):
    incl = (total, state)
    excl = (jnp.zeros_like(total), jnp.zeros_like(state))
    shift = 1
    while shift < count:
        perm = [(i, i + shift) for i in range(count - shift)]
        got_total, got_state = unpack_state(lax.ppermute(pack_state(*incl), axes, perm))
        excl = (got_total + excl[0], jnp.exp(excl[0])[:, None, None] * got_state + excl[1])
        if shift * 2 < count:
            incl = (got_total + incl[0], jnp.exp(incl[0])[:, None, None] * got_state + incl[1])
        shift *= 2
    return excl[1]


def attend_blocks(queries, own_keys, own_values, far_keys, far_values):
    score_scale = 1.0 / math.sqrt(P_SIZE)
    own_scores = (
        jnp.einsum("hbqd,hbkd->hbqk", queries, own_keys, preferred_element_type=f32) * score_scale
    )
    far_scores = (
        jnp.einsum("hbqd,hbkd->hbqk", queries, far_keys, preferred_element_type=f32) * score_scale
    )
    peak = jnp.maximum(
        jnp.max(own_scores, axis=-1, keepdims=True), jnp.max(far_scores, axis=-1, keepdims=True)
    )
    own_exp = jnp.exp(own_scores - peak)
    far_exp = jnp.exp(far_scores - peak)
    denominator = jnp.sum(own_exp, axis=-1, keepdims=True) + jnp.sum(
        far_exp, axis=-1, keepdims=True
    )
    own_weight = (own_exp / denominator).astype(bf16)
    far_weight = (far_exp / denominator).astype(bf16)
    mixed = jnp.einsum("hbqk,hbkd->hbqd", own_weight, own_values, preferred_element_type=f32)
    mixed = mixed + jnp.einsum(
        "hbqk,hbkd->hbqd", far_weight, far_values, preferred_element_type=f32
    )
    return mixed.astype(bf16)


def slot_ranks(owner_row, seq_count):
    owners_axis = jnp.arange(seq_count, dtype=jnp.int32)
    hits = (owner_row[:, None] == owners_axis[None, :]).astype(jnp.int32)
    return jnp.sum((jnp.cumsum(hits, axis=0) - hits) * hits, axis=1)


def per_device(
    tokens,
    norm_gain1,
    w_xz,
    w_bc,
    w_dt,
    dt_bias,
    decay_rate,
    curve_jump,
    skip_gain,
    norm_gain2,
    w_out,
    norm_gain3,
    w_q,
    w_kv,
    w_o,
    nbr_owner,
    nbr_block,
):
    token_count, width = tokens.shape
    seq_count = lax.axis_size("seq")
    device_count = lax.axis_size("grp") * seq_count
    block_count = token_count // BL
    request_count = block_count * KN
    slot_count = max(2, -(-request_count // seq_count))

    owner_flat = nbr_owner.reshape(-1)
    block_flat = nbr_block.reshape(-1)
    own_rank = slot_ranks(owner_flat, seq_count)
    targets = jnp.arange(seq_count, dtype=jnp.int32)[:, None, None]
    slots = jnp.arange(slot_count, dtype=jnp.int32)[None, :, None]
    match = (owner_flat[None, None, :] == targets) & (own_rank[None, None, :] == slots)
    wanted = jnp.sum(jnp.where(match, block_flat[None, None, :], 0), axis=2)
    send_index = lax.all_to_all(wanted, "seq", split_axis=0, concat_axis=0, tiled=True)
    arrival_index = owner_flat * slot_count + own_rank

    normed1 = rms_rows(tokens, norm_gain1)
    x = heads_of(normed1, w_xz[:, :INNER])
    z = heads_of(normed1, w_xz[:, INNER:])
    maps = jnp.dot(normed1, w_bc, preferred_element_type=f32).astype(bf16)
    dt = jnp.einsum("td,dh->ht", normed1, w_dt, preferred_element_type=f32)
    u = jax.nn.softplus(dt + dt_bias[:, None])
    log_decay = -(decay_rate[:, None] * u + curve_jump[None, :])
    y_intra, prefix, before, local_state, local_total, running, cc = chunk_parts(
        x, maps[:, :NS], maps[:, NS:], u, log_decay
    )
    entering = device_prefix(local_total, local_state, ("grp", "seq"), device_count)
    chunk_in = jnp.exp(before)[:, :, None, None] * entering[:, None] + prefix
    arriving = jnp.einsum("ctn,hcpn->hctp", cc.astype(f32), chunk_in, precision=highest)
    ssm = (y_intra + jnp.exp(running)[..., None] * arriving).reshape(H, token_count, P_SIZE)

    total = ssm + skip_gain[:, None, None] * x.astype(f32)
    gated = total * jax.nn.silu(z.astype(f32))
    head_normed = gated * lax.rsqrt(jnp.mean(gated * gated, axis=-1, keepdims=True) + epsilon)
    scaled = (head_normed * norm_gain2.reshape(H, 1, P_SIZE)).astype(bf16)
    middle = (
        tokens.astype(f32)
        + jnp.einsum(
            "htp,hpd->td", scaled, w_out.reshape(H, P_SIZE, width), preferred_element_type=f32
        )
    ).astype(bf16)

    normed = rms_rows(middle, norm_gain3)
    own_rows = normed.reshape(block_count, BL, width)
    outgoing = own_rows[send_index]
    arrived = lax.all_to_all(outgoing, "seq", split_axis=0, concat_axis=0, tiled=True)
    far_rows = arrived.reshape(seq_count * slot_count, BL, width)[arrival_index]
    far_rows = far_rows.reshape(request_count * BL, width)

    queries = heads_of(normed, w_q).reshape(H, block_count, BL, P_SIZE)
    own_keys = heads_of(normed, w_kv[:, :INNER]).reshape(H, block_count, BL, P_SIZE)
    own_values = heads_of(normed, w_kv[:, INNER:]).reshape(H, block_count, BL, P_SIZE)
    far_keys = heads_of(far_rows, w_kv[:, :INNER]).reshape(H, block_count, KN * BL, P_SIZE)
    far_values = heads_of(far_rows, w_kv[:, INNER:]).reshape(H, block_count, KN * BL, P_SIZE)
    attended = attend_blocks(queries, own_keys, own_values, far_keys, far_values)
    attended = attended.reshape(H, token_count, P_SIZE)
    return (
        middle.astype(f32)
        + jnp.einsum(
            "hte,hed->td", attended, w_o.reshape(H, P_SIZE, width), preferred_element_type=f32
        )
    ).astype(bf16)


def solution(mesh):
    in_specs = (
        P(("grp", "seq"), None),
        P(),
        P(),
        P(),
        P(),
        P(),
        P(),
        P(("grp", "seq")),
        P(),
        P(),
        P(),
        P(),
        P(),
        P(),
        P(),
        P(("grp", "seq"), None),
        P(("grp", "seq"), None),
    )
    out_specs = P(("grp", "seq"), None)
    return jax.shard_map(
        per_device, mesh=mesh, in_specs=in_specs, out_specs=out_specs, check_vma=False
    )
```

```python
import math

import jax
import jax.numpy as jnp
from jax import lax
from jax.sharding import PartitionSpec as P

H = 16
P_SIZE = 64
NS = 128
INNER = 1024
CH = 128
BL = 64
KN = 2


epsilon = 1e-05
highest = lax.Precision.HIGHEST
f32 = jnp.float32
bf16 = jnp.bfloat16
def rms_rows(values, weights):
    floats = values.astype(f32)
    return (
        floats * lax.rsqrt(jnp.mean(floats * floats, axis=-1, keepdims=True) + epsilon) * weights
    ).astype(bf16)


def heads_of(rows, weight):
    split = weight.reshape(weight.shape[0], H, P_SIZE)
    return jnp.einsum("td,dhe->hte", rows, split, preferred_element_type=f32).astype(bf16)


def chunk_parts(x, b, c, u, log_decay):
    count = x.shape[1] // CH
    xc = x.reshape(H, count, CH, P_SIZE)
    bc = b.reshape(count, CH, NS)
    cc = c.reshape(count, CH, NS)
    uc = u.reshape(H, count, CH)
    running = jnp.cumsum(log_decay.reshape(H, count, CH), axis=2)
    lower = (jnp.arange(CH)[:, None] >= jnp.arange(CH)[None, :])[None, None]
    spread = running[..., :, None] - running[..., None, :]
    weights = jnp.where(lower, jnp.exp(jnp.where(lower, spread, 0.0)), 0.0)
    intersection = jnp.einsum("ctn,csn->cts", cc, bc, preferred_element_type=f32)
    mixing = (intersection[None] * weights * uc[:, :, None, :]).astype(bf16)
    y_intra = jnp.einsum("hcts,hcsp->hctp", mixing, xc, preferred_element_type=f32)
    last = running[..., -1]
    tail_weight = jnp.exp(last[..., None] - running) * uc
    tail = (tail_weight[..., None] * xc.astype(f32)).astype(bf16)
    chunk_state = jnp.einsum("hcsp,csn->hcpn", tail, bc, preferred_element_type=f32)
    prefix = [jnp.zeros((H, P_SIZE, NS), f32)]
    before = [jnp.zeros((H,), f32)]
    for k in range(count):
        prefix.append(jnp.exp(last[:, k])[:, None, None] * prefix[-1] + chunk_state[:, k])
        before.append(before[-1] + last[:, k])
    return (
        y_intra,
        jnp.stack(prefix[:count], axis=1),
        jnp.stack(before[:count], axis=1),
        prefix[count],
        before[count],
        running,
        cc,
    )


def to_wire(total, state):
    high = total.astype(bf16)
    rest = total - high.astype(f32)
    middle = rest.astype(bf16)
    low = (rest - middle.astype(f32)).astype(bf16)
    pieces = jnp.pad(jnp.stack([high, middle, low]), ((0, 5), (0, NS - H)))
    return jnp.concatenate([state.reshape(H * P_SIZE, NS).astype(bf16), pieces], axis=0)


def from_wire(wire):
    pieces = wire[H * P_SIZE : H * P_SIZE + 3, :H].astype(f32)
    total = pieces[0] + pieces[1] + pieces[2]
    return total, wire[: H * P_SIZE].astype(f32).reshape(H, P_SIZE, NS)


def link(earlier, later):
    return (earlier[0] + later[0], jnp.exp(later[0])[:, None, None] * earlier[1] + later[1])


def device_prefix(total, state, axes, count, radix=4):
    incl = (total, state)
    excl = (jnp.zeros_like(total), jnp.zeros_like(state))
    span = 1
    while span < count:
        wire = to_wire(*incl)
        got = None
        for step in range(1, radix):
            shift = step * span
            if shift >= count:
                break
            perm = [(i, i + shift) for i in range(count - shift)]
            part = from_wire(lax.ppermute(wire, axes, perm))
            got = part if got is None else link(part, got)
        excl = link(got, excl)
        if span * radix < count:
            incl = link(got, incl)
        span *= radix
    return excl[1]


def attend_blocks(queries, own_keys, own_values, far_keys, far_values):
    score_scale = 1.0 / math.sqrt(P_SIZE)
    own_scores = (
        jnp.einsum("hbqd,hbkd->hbqk", queries, own_keys, preferred_element_type=f32) * score_scale
    )
    far_scores = (
        jnp.einsum("hbqd,hbkd->hbqk", queries, far_keys, preferred_element_type=f32) * score_scale
    )
    peak = jnp.maximum(
        jnp.max(own_scores, axis=-1, keepdims=True), jnp.max(far_scores, axis=-1, keepdims=True)
    )
    own_exp = jnp.exp(own_scores - peak)
    far_exp = jnp.exp(far_scores - peak)
    denominator = jnp.sum(own_exp, axis=-1, keepdims=True) + jnp.sum(
        far_exp, axis=-1, keepdims=True
    )
    own_weight = (own_exp / denominator).astype(bf16)
    far_weight = (far_exp / denominator).astype(bf16)
    mixed = jnp.einsum("hbqk,hbkd->hbqd", own_weight, own_values, preferred_element_type=f32)
    mixed = mixed + jnp.einsum(
        "hbqk,hbkd->hbqd", far_weight, far_values, preferred_element_type=f32
    )
    return mixed.astype(bf16)


def slot_ranks(owner_row, seq_count):
    owners_axis = jnp.arange(seq_count, dtype=jnp.int32)
    hits = (owner_row[:, None] == owners_axis[None, :]).astype(jnp.int32)
    return jnp.sum((jnp.cumsum(hits, axis=0) - hits) * hits, axis=1)


def per_device(
    tokens,
    norm_gain1,
    w_xz,
    w_bc,
    w_dt,
    dt_bias,
    decay_rate,
    curve_jump,
    skip_gain,
    norm_gain2,
    w_out,
    norm_gain3,
    w_q,
    w_kv,
    w_o,
    nbr_owner,
    nbr_block,
):
    token_count, width = tokens.shape
    seq_count = lax.axis_size("seq")
    device_count = lax.axis_size("grp") * seq_count
    block_count = token_count // BL
    request_count = block_count * KN
    slot_count = max(2, -(-request_count // seq_count))

    owner_flat = nbr_owner.reshape(-1)
    block_flat = nbr_block.reshape(-1)
    own_rank = slot_ranks(owner_flat, seq_count)
    targets = jnp.arange(seq_count, dtype=jnp.int32)[:, None, None]
    slots = jnp.arange(slot_count, dtype=jnp.int32)[None, :, None]
    match = (owner_flat[None, None, :] == targets) & (own_rank[None, None, :] == slots)
    wanted = jnp.sum(jnp.where(match, block_flat[None, None, :], 0), axis=2)
    send_index = lax.all_to_all(wanted, "seq", split_axis=0, concat_axis=0, tiled=True)
    arrival_index = owner_flat * slot_count + own_rank

    normed1 = rms_rows(tokens, norm_gain1)
    x = heads_of(normed1, w_xz[:, :INNER])
    z = heads_of(normed1, w_xz[:, INNER:])
    maps = jnp.dot(normed1, w_bc, preferred_element_type=f32).astype(bf16)
    dt = jnp.einsum("td,dh->ht", normed1, w_dt, preferred_element_type=f32)
    u = jax.nn.softplus(dt + dt_bias[:, None])
    log_decay = -(decay_rate[:, None] * u + curve_jump[None, :])
    y_intra, prefix, before, local_state, local_total, running, cc = chunk_parts(
        x, maps[:, :NS], maps[:, NS:], u, log_decay
    )
    entering = device_prefix(local_total, local_state, ("grp", "seq"), device_count)
    chunk_in = jnp.exp(before)[:, :, None, None] * entering[:, None] + prefix
    arriving = jnp.einsum("ctn,hcpn->hctp", cc.astype(f32), chunk_in, precision=highest)
    ssm = (y_intra + jnp.exp(running)[..., None] * arriving).reshape(H, token_count, P_SIZE)

    total = ssm + skip_gain[:, None, None] * x.astype(f32)
    gated = total * jax.nn.silu(z.astype(f32))
    head_normed = gated * lax.rsqrt(jnp.mean(gated * gated, axis=-1, keepdims=True) + epsilon)
    scaled = (head_normed * norm_gain2.reshape(H, 1, P_SIZE)).astype(bf16)
    middle = (
        tokens.astype(f32)
        + jnp.einsum(
            "htp,hpd->td", scaled, w_out.reshape(H, P_SIZE, width), preferred_element_type=f32
        )
    ).astype(bf16)

    normed = rms_rows(middle, norm_gain3)
    own_rows = normed.reshape(block_count, BL, width)
    outgoing = own_rows[send_index]
    arrived = lax.all_to_all(outgoing, "seq", split_axis=0, concat_axis=0, tiled=True)
    far_rows = arrived.reshape(seq_count * slot_count, BL, width)[arrival_index]
    far_rows = far_rows.reshape(request_count * BL, width)

    queries = heads_of(normed, w_q).reshape(H, block_count, BL, P_SIZE)
    own_keys = heads_of(normed, w_kv[:, :INNER]).reshape(H, block_count, BL, P_SIZE)
    own_values = heads_of(normed, w_kv[:, INNER:]).reshape(H, block_count, BL, P_SIZE)
    far_keys = heads_of(far_rows, w_kv[:, :INNER]).reshape(H, block_count, KN * BL, P_SIZE)
    far_values = heads_of(far_rows, w_kv[:, INNER:]).reshape(H, block_count, KN * BL, P_SIZE)
    attended = attend_blocks(queries, own_keys, own_values, far_keys, far_values)
    attended = attended.reshape(H, token_count, P_SIZE)
    return (
        middle.astype(f32)
        + jnp.einsum(
            "hte,hed->td", attended, w_o.reshape(H, P_SIZE, width), preferred_element_type=f32
        )
    ).astype(bf16)


def solution(mesh):
    in_specs = (
        P(("grp", "seq"), None),
        P(),
        P(),
        P(),
        P(),
        P(),
        P(),
        P(("grp", "seq")),
        P(),
        P(),
        P(),
        P(),
        P(),
        P(),
        P(),
        P(("grp", "seq"), None),
        P(("grp", "seq"), None),
    )
    out_specs = P(("grp", "seq"), None)
    return jax.shard_map(
        per_device, mesh=mesh, in_specs=in_specs, out_specs=out_specs, check_vma=False
    )
```

```python
import math

import jax
import jax.numpy as jnp
from jax import lax
from jax.experimental import pallas as pl
from jax.sharding import PartitionSpec as P

H = 16
P_SIZE = 64
NS = 128
INNER = 1024
CH = 128
BL = 64
KN = 2


epsilon = 1e-05
highest = lax.Precision.HIGHEST
f32 = jnp.float32
bf16 = jnp.bfloat16
def rms_rows(values, weights):
    floats = values.astype(f32)
    return (
        floats * lax.rsqrt(jnp.mean(floats * floats, axis=-1, keepdims=True) + epsilon) * weights
    ).astype(bf16)


def heads_of(rows, weight):
    split = weight.reshape(weight.shape[0], H, P_SIZE)
    return jnp.einsum("td,dhe->hte", rows, split, preferred_element_type=f32).astype(bf16)


def chunk_parts(x, b, c, u, log_decay):
    count = x.shape[1] // CH
    xc = x.reshape(H, count, CH, P_SIZE)
    bc = b.reshape(count, CH, NS)
    cc = c.reshape(count, CH, NS)
    uc = u.reshape(H, count, CH)
    running = jnp.cumsum(log_decay.reshape(H, count, CH), axis=2)
    lower = (jnp.arange(CH)[:, None] >= jnp.arange(CH)[None, :])[None, None]
    spread = running[..., :, None] - running[..., None, :]
    weights = jnp.where(lower, jnp.exp(jnp.where(lower, spread, 0.0)), 0.0)
    intersection = jnp.einsum("ctn,csn->cts", cc, bc, preferred_element_type=f32)
    mixing = (intersection[None] * weights * uc[:, :, None, :]).astype(bf16)
    y_intra = jnp.einsum("hcts,hcsp->hctp", mixing, xc, preferred_element_type=f32)
    last = running[..., -1]
    tail_weight = jnp.exp(last[..., None] - running) * uc
    tail = (tail_weight[..., None] * xc.astype(f32)).astype(bf16)
    chunk_state = jnp.einsum("hcsp,csn->hcpn", tail, bc, preferred_element_type=f32)
    prefix = [jnp.zeros((H, P_SIZE, NS), f32)]
    before = [jnp.zeros((H,), f32)]
    for k in range(count):
        prefix.append(jnp.exp(last[:, k])[:, None, None] * prefix[-1] + chunk_state[:, k])
        before.append(before[-1] + last[:, k])
    return (
        y_intra,
        jnp.stack(prefix[:count], axis=1),
        jnp.stack(before[:count], axis=1),
        prefix[count],
        before[count],
        running,
        cc,
    )


def to_wire(total, state):
    high = total.astype(bf16)
    rest = total - high.astype(f32)
    middle = rest.astype(bf16)
    low = (rest - middle.astype(f32)).astype(bf16)
    pieces = jnp.pad(jnp.stack([high, middle, low]), ((0, 5), (0, NS - H)))
    return jnp.concatenate([state.reshape(H * P_SIZE, NS).astype(bf16), pieces], axis=0)


def from_wire(wire):
    pieces = wire[H * P_SIZE : H * P_SIZE + 3, :H].astype(f32)
    total = pieces[0] + pieces[1] + pieces[2]
    return total, wire[: H * P_SIZE].astype(f32).reshape(H, P_SIZE, NS)


def link(earlier, later):
    return (earlier[0] + later[0], jnp.exp(later[0])[:, None, None] * earlier[1] + later[1])


def device_prefix(total, state, axes, count, radix=4):
    incl = (total, state)
    excl = (jnp.zeros_like(total), jnp.zeros_like(state))
    span = 1
    while span < count:
        wire = to_wire(*incl)
        got = None
        for step in range(1, radix):
            shift = step * span
            if shift >= count:
                break
            perm = [(i, i + shift) for i in range(count - shift)]
            part = from_wire(lax.ppermute(wire, axes, perm))
            got = part if got is None else link(part, got)
        excl = link(got, excl)
        if span * radix < count:
            incl = link(got, incl)
        span *= radix
    return excl[1]


def attention_kernel(q_ref, own_ref, far_ref, out_ref):
    score_scale = 1.0 / math.sqrt(P_SIZE)
    pair = 2 * P_SIZE
    lane = lax.broadcasted_iota(jnp.int32, (q_ref.shape[0], pair), 1)
    first = lane < P_SIZE
    contract = (((1,), (1,)), ((), ()))
    for p in range(INNER // pair):
        keys = slice(p * pair, (p + 1) * pair)
        values = slice(INNER + p * pair, INNER + (p + 1) * pair)
        both = q_ref[:, keys]
        own_keys = own_ref[:, keys]
        far_keys = far_ref[:, keys]
        own_values = own_ref[:, values]
        far_values = far_ref[:, values]
        halves = []
        for mask in (first, jnp.logical_not(first)):
            query = jnp.where(mask, both, jnp.zeros_like(both))
            own_scores = lax.dot_general(query, own_keys, contract, preferred_element_type=f32)
            far_scores = lax.dot_general(query, far_keys, contract, preferred_element_type=f32)
            own_scores = own_scores * score_scale
            far_scores = far_scores * score_scale
            peak = jnp.maximum(
                jnp.max(own_scores, axis=-1, keepdims=True),
                jnp.max(far_scores, axis=-1, keepdims=True),
            )
            own_exp = jnp.exp(own_scores - peak)
            far_exp = jnp.exp(far_scores - peak)
            denominator = jnp.sum(own_exp, axis=-1, keepdims=True) + jnp.sum(
                far_exp, axis=-1, keepdims=True
            )
            own_weight = (own_exp / denominator).astype(bf16)
            far_weight = (far_exp / denominator).astype(bf16)
            mixed = jnp.dot(own_weight, own_values, preferred_element_type=f32)
            mixed = mixed + jnp.dot(far_weight, far_values, preferred_element_type=f32)
            halves.append(mixed)
        out_ref[:, keys] = jnp.where(first, halves[0], halves[1]).astype(bf16)


def attend_blocks(queries, own_kv, far_kv):
    block_count = queries.shape[0] // BL
    far_rows = far_kv.shape[0] // block_count
    flops = 2 * 2 * queries.shape[0] * (BL + far_rows) * INNER * 2
    moved = 2 * (queries.size * 2 + own_kv.size + far_kv.size)
    return pl.pallas_call(
        attention_kernel,
        grid=(block_count,),
        in_specs=[
            pl.BlockSpec((BL, INNER), lambda b: (b, 0)),
            pl.BlockSpec((BL, 2 * INNER), lambda b: (b, 0)),
            pl.BlockSpec((far_rows, 2 * INNER), lambda b: (b, 0)),
        ],
        out_specs=pl.BlockSpec((BL, INNER), lambda b: (b, 0)),
        out_shape=jax.ShapeDtypeStruct((queries.shape[0], INNER), bf16),
        cost_estimate=pl.CostEstimate(
            flops=flops, transcendentals=queries.shape[0] * (BL + far_rows) * H * 2,
            bytes_accessed=moved,
        ),
    )(queries, own_kv, far_kv)


def slot_ranks(owner_row, seq_count):
    owners_axis = jnp.arange(seq_count, dtype=jnp.int32)
    hits = (owner_row[:, None] == owners_axis[None, :]).astype(jnp.int32)
    return jnp.sum((jnp.cumsum(hits, axis=0) - hits) * hits, axis=1)


def per_device(
    tokens,
    norm_gain1,
    w_xz,
    w_bc,
    w_dt,
    dt_bias,
    decay_rate,
    curve_jump,
    skip_gain,
    norm_gain2,
    w_out,
    norm_gain3,
    w_q,
    w_kv,
    w_o,
    nbr_owner,
    nbr_block,
):
    token_count, width = tokens.shape
    seq_count = lax.axis_size("seq")
    device_count = lax.axis_size("grp") * seq_count
    block_count = token_count // BL
    request_count = block_count * KN
    slot_count = max(2, -(-request_count // seq_count))

    owner_flat = nbr_owner.reshape(-1)
    block_flat = nbr_block.reshape(-1)
    own_rank = slot_ranks(owner_flat, seq_count)
    targets = jnp.arange(seq_count, dtype=jnp.int32)[:, None, None]
    slots = jnp.arange(slot_count, dtype=jnp.int32)[None, :, None]
    match = (owner_flat[None, None, :] == targets) & (own_rank[None, None, :] == slots)
    wanted = jnp.sum(jnp.where(match, block_flat[None, None, :], 0), axis=2)
    send_index = lax.all_to_all(wanted, "seq", split_axis=0, concat_axis=0, tiled=True)
    arrival_index = owner_flat * slot_count + own_rank

    normed1 = rms_rows(tokens, norm_gain1)
    x = heads_of(normed1, w_xz[:, :INNER])
    z = heads_of(normed1, w_xz[:, INNER:])
    maps = jnp.dot(normed1, w_bc, preferred_element_type=f32).astype(bf16)
    dt = jnp.einsum("td,dh->ht", normed1, w_dt, preferred_element_type=f32)
    u = jax.nn.softplus(dt + dt_bias[:, None])
    log_decay = -(decay_rate[:, None] * u + curve_jump[None, :])
    y_intra, prefix, before, local_state, local_total, running, cc = chunk_parts(
        x, maps[:, :NS], maps[:, NS:], u, log_decay
    )
    entering = device_prefix(local_total, local_state, ("grp", "seq"), device_count)
    chunk_in = jnp.exp(before)[:, :, None, None] * entering[:, None] + prefix
    arriving = jnp.einsum("ctn,hcpn->hctp", cc.astype(f32), chunk_in, precision=highest)
    ssm = (y_intra + jnp.exp(running)[..., None] * arriving).reshape(H, token_count, P_SIZE)

    total = ssm + skip_gain[:, None, None] * x.astype(f32)
    gated = total * jax.nn.silu(z.astype(f32))
    head_normed = gated * lax.rsqrt(jnp.mean(gated * gated, axis=-1, keepdims=True) + epsilon)
    scaled = (head_normed * norm_gain2.reshape(H, 1, P_SIZE)).astype(bf16)
    middle = (
        tokens.astype(f32)
        + jnp.einsum(
            "htp,hpd->td", scaled, w_out.reshape(H, P_SIZE, width), preferred_element_type=f32
        )
    ).astype(bf16)

    normed = rms_rows(middle, norm_gain3)
    own_rows = normed.reshape(block_count, BL, width)
    outgoing = own_rows[send_index]
    arrived = lax.all_to_all(outgoing, "seq", split_axis=0, concat_axis=0, tiled=True)
    far_rows = arrived.reshape(seq_count * slot_count, BL, width)[arrival_index]
    far_rows = far_rows.reshape(request_count * BL, width)

    queries = jnp.dot(normed, w_q, preferred_element_type=f32).astype(bf16)
    own_kv = jnp.dot(normed, w_kv, preferred_element_type=f32).astype(bf16)
    far_kv = jnp.dot(far_rows, w_kv, preferred_element_type=f32).astype(bf16)
    attended = attend_blocks(queries, own_kv, far_kv)
    return (
        middle.astype(f32)
        + jnp.dot(attended, w_o, preferred_element_type=f32)
    ).astype(bf16)


def solution(mesh):
    in_specs = (
        P(("grp", "seq"), None),
        P(),
        P(),
        P(),
        P(),
        P(),
        P(),
        P(("grp", "seq")),
        P(),
        P(),
        P(),
        P(),
        P(),
        P(),
        P(),
        P(("grp", "seq"), None),
        P(("grp", "seq"), None),
    )
    out_specs = P(("grp", "seq"), None)
    return jax.shard_map(
        per_device, mesh=mesh, in_specs=in_specs, out_specs=out_specs, check_vma=False
    )
```

```python
import math

import jax
import jax.numpy as jnp
from jax import lax
from jax.sharding import PartitionSpec as P

H = 16
P_SIZE = 64
NS = 128
INNER = 1024
CH = 128
BL = 64
KN = 2


epsilon = 1e-05
highest = lax.Precision.HIGHEST
f32 = jnp.float32
bf16 = jnp.bfloat16
def rms_rows(values, weights):
    floats = values.astype(f32)
    return (
        floats * lax.rsqrt(jnp.mean(floats * floats, axis=-1, keepdims=True) + epsilon) * weights
    ).astype(bf16)


def heads_of(rows, weight):
    flat = jnp.dot(rows, weight, preferred_element_type=f32).astype(bf16)
    return flat.reshape(rows.shape[0], H, P_SIZE).transpose(1, 0, 2)


def chunk_parts(x, b, c, u, log_decay):
    count = x.shape[1] // CH
    xc = x.reshape(H, count, CH, P_SIZE)
    bc = b.reshape(count, CH, NS)
    cc = c.reshape(count, CH, NS)
    uc = u.reshape(H, count, CH)
    running = jnp.cumsum(log_decay.reshape(H, count, CH), axis=2)
    lower = (jnp.arange(CH)[:, None] >= jnp.arange(CH)[None, :])[None, None]
    spread = running[..., :, None] - running[..., None, :]
    weights = jnp.where(lower, jnp.exp(jnp.where(lower, spread, 0.0)), 0.0)
    intersection = jnp.einsum("ctn,csn->cts", cc, bc, preferred_element_type=f32)
    mixing = (intersection[None] * weights * uc[:, :, None, :]).astype(bf16)
    y_intra = jnp.einsum("hcts,hcsp->hctp", mixing, xc, preferred_element_type=f32)
    last = running[..., -1]
    tail_weight = jnp.exp(last[..., None] - running) * uc
    tail = (tail_weight[..., None] * xc.astype(f32)).astype(bf16)
    chunk_state = jnp.einsum("hcsp,csn->hcpn", tail, bc, preferred_element_type=f32)
    prefix = [jnp.zeros((H, P_SIZE, NS), f32)]
    before = [jnp.zeros((H,), f32)]
    for k in range(count):
        prefix.append(jnp.exp(last[:, k])[:, None, None] * prefix[-1] + chunk_state[:, k])
        before.append(before[-1] + last[:, k])
    return (
        y_intra,
        jnp.stack(prefix[:count], axis=1),
        jnp.stack(before[:count], axis=1),
        prefix[count],
        before[count],
        running,
        cc,
    )


def to_wire(total, state):
    high = total.astype(bf16)
    rest = total - high.astype(f32)
    middle = rest.astype(bf16)
    low = (rest - middle.astype(f32)).astype(bf16)
    pieces = jnp.pad(jnp.stack([high, middle, low]), ((0, 5), (0, NS - H)))
    return jnp.concatenate([state.reshape(H * P_SIZE, NS).astype(bf16), pieces], axis=0)


def from_wire(wire):
    pieces = wire[H * P_SIZE : H * P_SIZE + 3, :H].astype(f32)
    total = pieces[0] + pieces[1] + pieces[2]
    return total, wire[: H * P_SIZE].astype(f32).reshape(H, P_SIZE, NS)


def link(earlier, later):
    return (earlier[0] + later[0], jnp.exp(later[0])[:, None, None] * earlier[1] + later[1])


def device_prefix(total, state, axes, count, radix=4):
    incl = (total, state)
    excl = (jnp.zeros_like(total), jnp.zeros_like(state))
    span = 1
    while span < count:
        wire = to_wire(*incl)
        got = None
        for step in range(1, radix):
            shift = step * span
            if shift >= count:
                break
            perm = [(i, i + shift) for i in range(count - shift)]
            part = from_wire(lax.ppermute(wire, axes, perm))
            got = part if got is None else link(part, got)
        excl = link(got, excl)
        if span * radix < count:
            incl = link(got, incl)
        span *= radix
    return excl[1]


def attend_blocks(queries, own_keys, own_values, far_keys, far_values):
    score_scale = 1.0 / math.sqrt(P_SIZE)
    own_scores = (
        jnp.einsum("hbqd,hbkd->hbqk", queries, own_keys, preferred_element_type=f32) * score_scale
    )
    far_scores = (
        jnp.einsum("hbqd,hbkd->hbqk", queries, far_keys, preferred_element_type=f32) * score_scale
    )
    peak = jnp.maximum(
        jnp.max(own_scores, axis=-1, keepdims=True), jnp.max(far_scores, axis=-1, keepdims=True)
    )
    own_exp = jnp.exp(own_scores - peak)
    far_exp = jnp.exp(far_scores - peak)
    denominator = jnp.sum(own_exp, axis=-1, keepdims=True) + jnp.sum(
        far_exp, axis=-1, keepdims=True
    )
    own_weight = (own_exp / denominator).astype(bf16)
    far_weight = (far_exp / denominator).astype(bf16)
    mixed = jnp.einsum("hbqk,hbkd->hbqd", own_weight, own_values, preferred_element_type=f32)
    mixed = mixed + jnp.einsum(
        "hbqk,hbkd->hbqd", far_weight, far_values, preferred_element_type=f32
    )
    return mixed.astype(bf16)


def slot_ranks(owner_row, seq_count):
    owners_axis = jnp.arange(seq_count, dtype=jnp.int32)
    hits = (owner_row[:, None] == owners_axis[None, :]).astype(jnp.int32)
    return jnp.sum((jnp.cumsum(hits, axis=0) - hits) * hits, axis=1)


def per_device(
    tokens,
    norm_gain1,
    w_xz,
    w_bc,
    w_dt,
    dt_bias,
    decay_rate,
    curve_jump,
    skip_gain,
    norm_gain2,
    w_out,
    norm_gain3,
    w_q,
    w_kv,
    w_o,
    nbr_owner,
    nbr_block,
):
    token_count, width = tokens.shape
    seq_count = lax.axis_size("seq")
    device_count = lax.axis_size("grp") * seq_count
    block_count = token_count // BL
    request_count = block_count * KN
    slot_count = max(2, -(-request_count // seq_count))

    owner_flat = nbr_owner.reshape(-1)
    block_flat = nbr_block.reshape(-1)
    own_rank = slot_ranks(owner_flat, seq_count)
    targets = jnp.arange(seq_count, dtype=jnp.int32)[:, None, None]
    slots = jnp.arange(slot_count, dtype=jnp.int32)[None, :, None]
    match = (owner_flat[None, None, :] == targets) & (own_rank[None, None, :] == slots)
    wanted = jnp.sum(jnp.where(match, block_flat[None, None, :], 0), axis=2)
    arrival_index = owner_flat * slot_count + own_rank

    normed1 = rms_rows(tokens, norm_gain1)
    x = heads_of(normed1, w_xz[:, :INNER])
    z = heads_of(normed1, w_xz[:, INNER:])
    maps = jnp.dot(normed1, w_bc, preferred_element_type=f32).astype(bf16)
    dt = jnp.einsum("td,dh->ht", normed1, w_dt, preferred_element_type=f32)
    u = jax.nn.softplus(dt + dt_bias[:, None])
    log_decay = -(decay_rate[:, None] * u + curve_jump[None, :])
    y_intra, prefix, before, local_state, local_total, running, cc = chunk_parts(
        x, maps[:, :NS], maps[:, NS:], u, log_decay
    )
    local_state, y_intra = lax.optimization_barrier((local_state, y_intra))
    entering = device_prefix(local_total, local_state, ("grp", "seq"), device_count)
    entering, wanted = lax.optimization_barrier((entering, wanted))
    send_index = lax.all_to_all(wanted, "seq", split_axis=0, concat_axis=0, tiled=True)
    chunk_in = jnp.exp(before)[:, :, None, None] * entering[:, None] + prefix
    arriving = jnp.einsum("ctn,hcpn->hctp", cc.astype(f32), chunk_in, precision=highest)
    ssm = (y_intra + jnp.exp(running)[..., None] * arriving).reshape(H, token_count, P_SIZE)

    total = ssm + skip_gain[:, None, None] * x.astype(f32)
    gated = total * jax.nn.silu(z.astype(f32))
    head_normed = gated * lax.rsqrt(jnp.mean(gated * gated, axis=-1, keepdims=True) + epsilon)
    scaled = (head_normed * norm_gain2.reshape(H, 1, P_SIZE)).astype(bf16)
    middle = (
        tokens.astype(f32)
        + jnp.einsum(
            "htp,hpd->td", scaled, w_out.reshape(H, P_SIZE, width), preferred_element_type=f32
        )
    ).astype(bf16)

    normed = rms_rows(middle, norm_gain3)
    own_rows = normed.reshape(block_count, BL, width)
    outgoing = own_rows[send_index]
    arrived = lax.all_to_all(outgoing, "seq", split_axis=0, concat_axis=0, tiled=True)
    far_rows = arrived.reshape(seq_count * slot_count, BL, width)[arrival_index]
    far_rows = far_rows.reshape(request_count * BL, width)

    queries = heads_of(normed, w_q).reshape(H, block_count, BL, P_SIZE)
    own_keys = heads_of(normed, w_kv[:, :INNER]).reshape(H, block_count, BL, P_SIZE)
    own_values = heads_of(normed, w_kv[:, INNER:]).reshape(H, block_count, BL, P_SIZE)
    far_keys = heads_of(far_rows, w_kv[:, :INNER]).reshape(H, block_count, KN * BL, P_SIZE)
    far_values = heads_of(far_rows, w_kv[:, INNER:]).reshape(H, block_count, KN * BL, P_SIZE)
    attended = attend_blocks(queries, own_keys, own_values, far_keys, far_values)
    attended = attended.reshape(H, token_count, P_SIZE)
    return (
        middle.astype(f32)
        + jnp.einsum(
            "hte,hed->td", attended, w_o.reshape(H, P_SIZE, width), preferred_element_type=f32
        )
    ).astype(bf16)


def solution(mesh):
    in_specs = (
        P(("grp", "seq"), None),
        P(),
        P(),
        P(),
        P(),
        P(),
        P(),
        P(("grp", "seq")),
        P(),
        P(),
        P(),
        P(),
        P(),
        P(),
        P(),
        P(("grp", "seq"), None),
        P(("grp", "seq"), None),
    )
    out_specs = P(("grp", "seq"), None)
    return jax.shard_map(
        per_device, mesh=mesh, in_specs=in_specs, out_specs=out_specs, check_vma=False
    )
```

```python
import math

import jax
import jax.numpy as jnp
from jax import lax
from jax.sharding import PartitionSpec as P

H = 16
P_SIZE = 64
NS = 128
INNER = 1024
CH = 128
BL = 64
KN = 2


epsilon = 1e-05
highest = lax.Precision.HIGHEST
f32 = jnp.float32
bf16 = jnp.bfloat16
SEQ = ("x", "y", "c")
CURVE = ("z", "x", "y", "c")
def rms_rows(values, weights):
    floats = values.astype(f32)
    return (
        floats * lax.rsqrt(jnp.mean(floats * floats, axis=-1, keepdims=True) + epsilon) * weights
    ).astype(bf16)


def heads_of(rows, weight):
    flat = jnp.dot(rows, weight, preferred_element_type=f32).astype(bf16)
    return flat.reshape(rows.shape[0], H, P_SIZE).transpose(1, 0, 2)


def chunk_parts(x, b, c, u, log_decay):
    count = x.shape[1] // CH
    xc = x.reshape(H, count, CH, P_SIZE)
    bc = b.reshape(count, CH, NS)
    cc = c.reshape(count, CH, NS)
    uc = u.reshape(H, count, CH)
    running = jnp.cumsum(log_decay.reshape(H, count, CH), axis=2)
    lower = (jnp.arange(CH)[:, None] >= jnp.arange(CH)[None, :])[None, None]
    spread = running[..., :, None] - running[..., None, :]
    weights = jnp.where(lower, jnp.exp(jnp.where(lower, spread, 0.0)), 0.0)
    intersection = jnp.einsum("ctn,csn->cts", cc, bc, preferred_element_type=f32)
    mixing = (intersection[None] * weights * uc[:, :, None, :]).astype(bf16)
    y_intra = jnp.einsum("hcts,hcsp->hctp", mixing, xc, preferred_element_type=f32)
    last = running[..., -1]
    tail_weight = jnp.exp(last[..., None] - running) * uc
    tail = (tail_weight[..., None] * xc.astype(f32)).astype(bf16)
    chunk_state = jnp.einsum("hcsp,csn->hcpn", tail, bc, preferred_element_type=f32)
    prefix = [jnp.zeros((H, P_SIZE, NS), f32)]
    before = [jnp.zeros((H,), f32)]
    for k in range(count):
        prefix.append(jnp.exp(last[:, k])[:, None, None] * prefix[-1] + chunk_state[:, k])
        before.append(before[-1] + last[:, k])
    return (
        y_intra,
        jnp.stack(prefix[:count], axis=1),
        jnp.stack(before[:count], axis=1),
        prefix[count],
        before[count],
        running,
        cc,
    )


def to_wire(total, state):
    high = total.astype(bf16)
    rest = total - high.astype(f32)
    middle = rest.astype(bf16)
    low = (rest - middle.astype(f32)).astype(bf16)
    pieces = jnp.pad(jnp.stack([high, middle, low]), ((0, 5), (0, NS - H)))
    return jnp.concatenate([state.reshape(H * P_SIZE, NS).astype(bf16), pieces], axis=0)


def from_wire(wire):
    pieces = wire[H * P_SIZE : H * P_SIZE + 3, :H].astype(f32)
    total = pieces[0] + pieces[1] + pieces[2]
    return total, wire[: H * P_SIZE].astype(f32).reshape(H, P_SIZE, NS)


def link(earlier, later):
    return (earlier[0] + later[0], jnp.exp(later[0])[:, None, None] * earlier[1] + later[1])


def level_scan(value, axes):
    members = lax.axis_size(axes)
    place = lax.axis_index(axes)
    everyone = lax.all_gather(to_wire(*value), axes)
    ahead = (jnp.zeros_like(value[0]), jnp.zeros_like(value[1]))
    whole = ahead
    for k in range(members):
        part = from_wire(everyone[k])
        joined = link(ahead, part)
        earlier = k < place
        ahead = (jnp.where(earlier, joined[0], ahead[0]), jnp.where(earlier, joined[1], ahead[1]))
        whole = link(whole, part)
    return ahead, whole


def device_prefix(total, state, levels):
    value = (total, state)
    aheads = []
    for axes in levels:
        ahead, value = level_scan(value, axes)
        aheads.append(ahead)
    entering = aheads[-1]
    for ahead in reversed(aheads[:-1]):
        entering = link(entering, ahead)
    return entering[1]


def attend_blocks(queries, own_keys, own_values, far_keys, far_values):
    score_scale = 1.0 / math.sqrt(P_SIZE)
    own_scores = (
        jnp.einsum("hbqd,hbkd->hbqk", queries, own_keys, preferred_element_type=f32) * score_scale
    )
    far_scores = (
        jnp.einsum("hbqd,hbkd->hbqk", queries, far_keys, preferred_element_type=f32) * score_scale
    )
    peak = jnp.maximum(
        jnp.max(own_scores, axis=-1, keepdims=True), jnp.max(far_scores, axis=-1, keepdims=True)
    )
    own_exp = jnp.exp(own_scores - peak)
    far_exp = jnp.exp(far_scores - peak)
    denominator = jnp.sum(own_exp, axis=-1, keepdims=True) + jnp.sum(
        far_exp, axis=-1, keepdims=True
    )
    own_weight = (own_exp / denominator).astype(bf16)
    far_weight = (far_exp / denominator).astype(bf16)
    mixed = jnp.einsum("hbqk,hbkd->hbqd", own_weight, own_values, preferred_element_type=f32)
    mixed = mixed + jnp.einsum(
        "hbqk,hbkd->hbqd", far_weight, far_values, preferred_element_type=f32
    )
    return mixed.astype(bf16)


def slot_ranks(owner_row, seq_count):
    owners_axis = jnp.arange(seq_count, dtype=jnp.int32)
    hits = (owner_row[:, None] == owners_axis[None, :]).astype(jnp.int32)
    return jnp.sum((jnp.cumsum(hits, axis=0) - hits) * hits, axis=1)


def per_device(
    tokens,
    norm_gain1,
    w_xz,
    w_bc,
    w_dt,
    dt_bias,
    decay_rate,
    curve_jump,
    skip_gain,
    norm_gain2,
    w_out,
    norm_gain3,
    w_q,
    w_kv,
    w_o,
    nbr_owner,
    nbr_block,
):
    token_count, width = tokens.shape
    seq_count = lax.axis_size(SEQ)
    block_count = token_count // BL
    request_count = block_count * KN
    slot_count = max(2, -(-request_count // seq_count))

    owner_flat = nbr_owner.reshape(-1)
    block_flat = nbr_block.reshape(-1)
    own_rank = slot_ranks(owner_flat, seq_count)
    targets = jnp.arange(seq_count, dtype=jnp.int32)[:, None, None]
    slots = jnp.arange(slot_count, dtype=jnp.int32)[None, :, None]
    match = (owner_flat[None, None, :] == targets) & (own_rank[None, None, :] == slots)
    wanted = jnp.sum(jnp.where(match, block_flat[None, None, :], 0), axis=2)
    send_index = lax.all_to_all(wanted, SEQ, split_axis=0, concat_axis=0, tiled=True)
    arrival_index = owner_flat * slot_count + own_rank

    normed1 = rms_rows(tokens, norm_gain1)
    x = heads_of(normed1, w_xz[:, :INNER])
    z = heads_of(normed1, w_xz[:, INNER:])
    maps = jnp.dot(normed1, w_bc, preferred_element_type=f32).astype(bf16)
    dt = jnp.einsum("td,dh->ht", normed1, w_dt, preferred_element_type=f32)
    u = jax.nn.softplus(dt + dt_bias[:, None])
    log_decay = -(decay_rate[:, None] * u + curve_jump[None, :])
    y_intra, prefix, before, local_state, local_total, running, cc = chunk_parts(
        x, maps[:, :NS], maps[:, NS:], u, log_decay
    )
    entering = device_prefix(local_total, local_state, (("y", "c"), ("x",), ("z",)))
    chunk_in = jnp.exp(before)[:, :, None, None] * entering[:, None] + prefix
    arriving = jnp.einsum("ctn,hcpn->hctp", cc.astype(f32), chunk_in, precision=highest)
    ssm = (y_intra + jnp.exp(running)[..., None] * arriving).reshape(H, token_count, P_SIZE)

    total = ssm + skip_gain[:, None, None] * x.astype(f32)
    gated = total * jax.nn.silu(z.astype(f32))
    head_normed = gated * lax.rsqrt(jnp.mean(gated * gated, axis=-1, keepdims=True) + epsilon)
    scaled = (head_normed * norm_gain2.reshape(H, 1, P_SIZE)).astype(bf16)
    middle = (
        tokens.astype(f32)
        + jnp.einsum(
            "htp,hpd->td", scaled, w_out.reshape(H, P_SIZE, width), preferred_element_type=f32
        )
    ).astype(bf16)

    normed = rms_rows(middle, norm_gain3)
    own_rows = normed.reshape(block_count, BL, width)
    outgoing = own_rows[send_index]
    arrived = lax.all_to_all(outgoing, SEQ, split_axis=0, concat_axis=0, tiled=True)
    far_rows = arrived.reshape(seq_count * slot_count, BL, width)[arrival_index]
    far_rows = far_rows.reshape(request_count * BL, width)

    queries = heads_of(normed, w_q).reshape(H, block_count, BL, P_SIZE)
    own_keys = heads_of(normed, w_kv[:, :INNER]).reshape(H, block_count, BL, P_SIZE)
    own_values = heads_of(normed, w_kv[:, INNER:]).reshape(H, block_count, BL, P_SIZE)
    far_keys = heads_of(far_rows, w_kv[:, :INNER]).reshape(H, block_count, KN * BL, P_SIZE)
    far_values = heads_of(far_rows, w_kv[:, INNER:]).reshape(H, block_count, KN * BL, P_SIZE)
    attended = attend_blocks(queries, own_keys, own_values, far_keys, far_values)
    attended = attended.reshape(H, token_count, P_SIZE)
    return (
        middle.astype(f32)
        + jnp.einsum(
            "hte,hed->td", attended, w_o.reshape(H, P_SIZE, width), preferred_element_type=f32
        )
    ).astype(bf16)


def solution(mesh):
    seq_shape = (mesh.shape["grp"], 4, mesh.shape["seq"] // 8, 2)
    fine = jax.sharding.Mesh(mesh.devices.reshape(seq_shape), CURVE)
    rows = P(CURVE, None)
    whole = P()
    in_specs = (rows, whole, whole, whole, whole, whole, whole, P(CURVE)) + (whole,) * 7 + (rows, rows)
    return jax.shard_map(
        per_device, mesh=fine, in_specs=in_specs, out_specs=rows, check_vma=False
    )
```

```python
import math

import jax
import jax.numpy as jnp
from jax import lax
from jax.sharding import PartitionSpec as P

H = 16
P_SIZE = 64
NS = 128
INNER = 1024
CH = 128
BL = 64
KN = 2


epsilon = 1e-05
highest = lax.Precision.HIGHEST
f32 = jnp.float32
bf16 = jnp.bfloat16
def rms_rows(values, weights):
    floats = values.astype(f32)
    return (
        floats * lax.rsqrt(jnp.mean(floats * floats, axis=-1, keepdims=True) + epsilon) * weights
    ).astype(bf16)


def heads_of(rows, weight):
    flat = jnp.dot(rows, weight, preferred_element_type=f32).astype(bf16)
    return flat.reshape(rows.shape[0], H, P_SIZE).transpose(1, 0, 2)


def chunk_parts(x, b, c, u, log_decay):
    count = x.shape[1] // CH
    xc = x.reshape(H, count, CH, P_SIZE)
    bc = b.reshape(count, CH, NS)
    cc = c.reshape(count, CH, NS)
    uc = u.reshape(H, count, CH)
    running = jnp.cumsum(log_decay.reshape(H, count, CH), axis=2)
    lower = (jnp.arange(CH)[:, None] >= jnp.arange(CH)[None, :])[None, None]
    spread = running[..., :, None] - running[..., None, :]
    weights = jnp.where(lower, jnp.exp(jnp.where(lower, spread, 0.0)), 0.0)
    intersection = jnp.einsum("ctn,csn->cts", cc, bc, preferred_element_type=f32)
    mixing = (intersection[None] * weights * uc[:, :, None, :]).astype(bf16)
    y_intra = jnp.einsum("hcts,hcsp->hctp", mixing, xc, preferred_element_type=f32)
    last = running[..., -1]
    tail_weight = jnp.exp(last[..., None] - running) * uc
    tail = (tail_weight[..., None] * xc.astype(f32)).astype(bf16)
    chunk_state = jnp.einsum("hcsp,csn->hcpn", tail, bc, preferred_element_type=f32)
    prefix = [jnp.zeros((H, P_SIZE, NS), f32)]
    before = [jnp.zeros((H,), f32)]
    for k in range(count):
        prefix.append(jnp.exp(last[:, k])[:, None, None] * prefix[-1] + chunk_state[:, k])
        before.append(before[-1] + last[:, k])
    return (
        y_intra,
        jnp.stack(prefix[:count], axis=1),
        jnp.stack(before[:count], axis=1),
        prefix[count],
        before[count],
        running,
        cc,
    )


def to_wire(total, state):
    high = total.astype(bf16)
    rest = total - high.astype(f32)
    middle = rest.astype(bf16)
    low = (rest - middle.astype(f32)).astype(bf16)
    pieces = jnp.pad(jnp.stack([high, middle, low]), ((0, 5), (0, NS - H)))
    return jnp.concatenate([state.reshape(H * P_SIZE, NS).astype(bf16), pieces], axis=0)


def from_wire(wire):
    pieces = wire[H * P_SIZE : H * P_SIZE + 3, :H].astype(f32)
    total = pieces[0] + pieces[1] + pieces[2]
    return total, wire[: H * P_SIZE].astype(f32).reshape(H, P_SIZE, NS)


def link(earlier, later):
    return (earlier[0] + later[0], jnp.exp(later[0])[:, None, None] * earlier[1] + later[1])


def device_prefix(total, state, axes, count, radix=4):
    incl = (total, state)
    excl = (jnp.zeros_like(total), jnp.zeros_like(state))
    span = 1
    while span < count:
        wire = to_wire(*incl)
        got = None
        for step in range(1, radix):
            shift = step * span
            if shift >= count:
                break
            perm = [(i, i + shift) for i in range(count - shift)]
            part = from_wire(lax.ppermute(wire, axes, perm))
            got = part if got is None else link(part, got)
        excl = link(got, excl)
        if span * radix < count:
            incl = link(got, incl)
        span *= radix
    return excl[1]


def attend_blocks(queries, own_keys, own_values, far_keys, far_values):
    score_scale = 1.0 / math.sqrt(P_SIZE)
    own_scores = (
        jnp.einsum("hbqd,hbkd->hbqk", queries, own_keys, preferred_element_type=f32) * score_scale
    )
    far_scores = (
        jnp.einsum("hbqd,hbkd->hbqk", queries, far_keys, preferred_element_type=f32) * score_scale
    )
    peak = jnp.maximum(
        jnp.max(own_scores, axis=-1, keepdims=True), jnp.max(far_scores, axis=-1, keepdims=True)
    )
    own_exp = jnp.exp(own_scores - peak)
    far_exp = jnp.exp(far_scores - peak)
    denominator = jnp.sum(own_exp, axis=-1, keepdims=True) + jnp.sum(
        far_exp, axis=-1, keepdims=True
    )
    own_weight = (own_exp / denominator).astype(bf16)
    far_weight = (far_exp / denominator).astype(bf16)
    mixed = jnp.einsum("hbqk,hbkd->hbqd", own_weight, own_values, preferred_element_type=f32)
    mixed = mixed + jnp.einsum(
        "hbqk,hbkd->hbqd", far_weight, far_values, preferred_element_type=f32
    )
    return mixed.astype(bf16)


def slot_ranks(owner_row, seq_count):
    owners_axis = jnp.arange(seq_count, dtype=jnp.int32)
    hits = (owner_row[:, None] == owners_axis[None, :]).astype(jnp.int32)
    return jnp.sum((jnp.cumsum(hits, axis=0) - hits) * hits, axis=1)


def per_device(
    tokens,
    norm_gain1,
    w_xz,
    w_bc,
    w_dt,
    dt_bias,
    decay_rate,
    curve_jump,
    skip_gain,
    norm_gain2,
    w_out,
    norm_gain3,
    w_q,
    w_kv,
    w_o,
    nbr_owner,
    nbr_block,
):
    token_count, width = tokens.shape
    seq_count = lax.axis_size("seq")
    device_count = lax.axis_size("grp") * seq_count
    block_count = token_count // BL
    request_count = block_count * KN
    slot_count = max(2, -(-request_count // seq_count))

    owner_flat = nbr_owner.reshape(-1)
    block_flat = nbr_block.reshape(-1)
    own_rank = slot_ranks(owner_flat, seq_count)
    targets = jnp.arange(seq_count, dtype=jnp.int32)[:, None, None]
    slots = jnp.arange(slot_count, dtype=jnp.int32)[None, :, None]
    match = (owner_flat[None, None, :] == targets) & (own_rank[None, None, :] == slots)
    wanted = jnp.sum(jnp.where(match, block_flat[None, None, :], 0), axis=2)
    arrival_index = owner_flat * slot_count + own_rank

    normed1 = rms_rows(tokens, norm_gain1)
    x = heads_of(normed1, w_xz[:, :INNER])
    z = heads_of(normed1, w_xz[:, INNER:])
    maps = jnp.dot(normed1, w_bc, preferred_element_type=f32).astype(bf16)
    dt = jnp.einsum("td,dh->ht", normed1, w_dt, preferred_element_type=f32)
    u = jax.nn.softplus(dt + dt_bias[:, None])
    log_decay = -(decay_rate[:, None] * u + curve_jump[None, :])
    y_intra, prefix, before, local_state, local_total, running, cc = chunk_parts(
        x, maps[:, :NS], maps[:, NS:], u, log_decay
    )
    send_index = lax.all_to_all(wanted, "seq", split_axis=0, concat_axis=0, tiled=True)
    local_state, y_intra, send_index = lax.optimization_barrier((local_state, y_intra, send_index))
    entering = device_prefix(local_total, local_state, ("grp", "seq"), device_count)
    chunk_in = jnp.exp(before)[:, :, None, None] * entering[:, None] + prefix
    arriving = jnp.einsum("ctn,hcpn->hctp", cc.astype(f32), chunk_in, precision=highest)
    ssm = (y_intra + jnp.exp(running)[..., None] * arriving).reshape(H, token_count, P_SIZE)

    total = ssm + skip_gain[:, None, None] * x.astype(f32)
    gated = total * jax.nn.silu(z.astype(f32))
    head_normed = gated * lax.rsqrt(jnp.mean(gated * gated, axis=-1, keepdims=True) + epsilon)
    scaled = (head_normed * norm_gain2.reshape(H, 1, P_SIZE)).astype(bf16)
    middle = (
        tokens.astype(f32)
        + jnp.einsum(
            "htp,hpd->td", scaled, w_out.reshape(H, P_SIZE, width), preferred_element_type=f32
        )
    ).astype(bf16)

    normed = rms_rows(middle, norm_gain3)
    own_rows = normed.reshape(block_count, BL, width)
    outgoing = own_rows[send_index]
    arrived = lax.all_to_all(outgoing, "seq", split_axis=0, concat_axis=0, tiled=True)
    far_rows = arrived.reshape(seq_count * slot_count, BL, width)[arrival_index]
    far_rows = far_rows.reshape(request_count * BL, width)

    queries = heads_of(normed, w_q).reshape(H, block_count, BL, P_SIZE)
    own_keys = heads_of(normed, w_kv[:, :INNER]).reshape(H, block_count, BL, P_SIZE)
    own_values = heads_of(normed, w_kv[:, INNER:]).reshape(H, block_count, BL, P_SIZE)
    far_keys = heads_of(far_rows, w_kv[:, :INNER]).reshape(H, block_count, KN * BL, P_SIZE)
    far_values = heads_of(far_rows, w_kv[:, INNER:]).reshape(H, block_count, KN * BL, P_SIZE)
    attended = attend_blocks(queries, own_keys, own_values, far_keys, far_values)
    attended = attended.reshape(H, token_count, P_SIZE)
    return (
        middle.astype(f32)
        + jnp.einsum(
            "hte,hed->td", attended, w_o.reshape(H, P_SIZE, width), preferred_element_type=f32
        )
    ).astype(bf16)


def solution(mesh):
    in_specs = (
        P(("grp", "seq"), None),
        P(),
        P(),
        P(),
        P(),
        P(),
        P(),
        P(("grp", "seq")),
        P(),
        P(),
        P(),
        P(),
        P(),
        P(),
        P(),
        P(("grp", "seq"), None),
        P(("grp", "seq"), None),
    )
    out_specs = P(("grp", "seq"), None)
    return jax.shard_map(
        per_device, mesh=mesh, in_specs=in_specs, out_specs=out_specs, check_vma=False
    )
```

```python
import math

import jax
import jax.numpy as jnp
from jax import lax
from jax.sharding import PartitionSpec as P

H = 16
P_SIZE = 64
NS = 128
INNER = 1024
CH = 128
BL = 64
KN = 2


epsilon = 1e-05
highest = lax.Precision.HIGHEST
f32 = jnp.float32
bf16 = jnp.bfloat16
SEQ = ("x", "y", "c")
CURVE = ("z", "x", "y", "c")
def rms_rows(values, weights):
    floats = values.astype(f32)
    return (
        floats * lax.rsqrt(jnp.mean(floats * floats, axis=-1, keepdims=True) + epsilon) * weights
    ).astype(bf16)


def heads_of(rows, weight):
    flat = jnp.dot(rows, weight, preferred_element_type=f32).astype(bf16)
    return flat.reshape(rows.shape[0], H, P_SIZE).transpose(1, 0, 2)


def chunk_parts(x, b, c, u, log_decay):
    count = x.shape[1] // CH
    xc = x.reshape(H, count, CH, P_SIZE)
    bc = b.reshape(count, CH, NS)
    cc = c.reshape(count, CH, NS)
    uc = u.reshape(H, count, CH)
    running = jnp.cumsum(log_decay.reshape(H, count, CH), axis=2)
    lower = (jnp.arange(CH)[:, None] >= jnp.arange(CH)[None, :])[None, None]
    spread = running[..., :, None] - running[..., None, :]
    weights = jnp.where(lower, jnp.exp(jnp.where(lower, spread, 0.0)), 0.0)
    intersection = jnp.einsum("ctn,csn->cts", cc, bc, preferred_element_type=f32)
    mixing = (intersection[None] * weights * uc[:, :, None, :]).astype(bf16)
    y_intra = jnp.einsum("hcts,hcsp->hctp", mixing, xc, preferred_element_type=f32)
    last = running[..., -1]
    tail_weight = jnp.exp(last[..., None] - running) * uc
    tail = (tail_weight[..., None] * xc.astype(f32)).astype(bf16)
    chunk_state = jnp.einsum("hcsp,csn->hcpn", tail, bc, preferred_element_type=f32)
    prefix = [jnp.zeros((H, P_SIZE, NS), f32)]
    before = [jnp.zeros((H,), f32)]
    for k in range(count):
        prefix.append(jnp.exp(last[:, k])[:, None, None] * prefix[-1] + chunk_state[:, k])
        before.append(before[-1] + last[:, k])
    return (
        y_intra,
        jnp.stack(prefix[:count], axis=1),
        jnp.stack(before[:count], axis=1),
        prefix[count],
        before[count],
        running,
        cc,
    )


def to_wire(total, state):
    high = total.astype(bf16)
    rest = total - high.astype(f32)
    middle = rest.astype(bf16)
    low = (rest - middle.astype(f32)).astype(bf16)
    pieces = jnp.pad(jnp.stack([high, middle, low]), ((0, 5), (0, NS - H)))
    return jnp.concatenate([state.reshape(H * P_SIZE, NS).astype(bf16), pieces], axis=0)


def from_wire(wire):
    pieces = wire[H * P_SIZE : H * P_SIZE + 3, :H].astype(f32)
    total = pieces[0] + pieces[1] + pieces[2]
    return total, wire[: H * P_SIZE].astype(f32).reshape(H, P_SIZE, NS)


def link(earlier, later):
    return (earlier[0] + later[0], jnp.exp(later[0])[:, None, None] * earlier[1] + later[1])


def level_scan(value, axes):
    members = lax.axis_size(axes)
    place = lax.axis_index(axes)
    wire = to_wire(*value)
    copies = jnp.broadcast_to(wire[None], (members,) + wire.shape)
    everyone = lax.all_to_all(copies, axes, split_axis=0, concat_axis=0, tiled=True)
    ahead = (jnp.zeros_like(value[0]), jnp.zeros_like(value[1]))
    whole = ahead
    for k in range(members):
        part = from_wire(everyone[k])
        joined = link(ahead, part)
        earlier = k < place
        ahead = (jnp.where(earlier, joined[0], ahead[0]), jnp.where(earlier, joined[1], ahead[1]))
        whole = link(whole, part)
    return ahead, whole


def device_prefix(total, state, levels):
    value = (total, state)
    aheads = []
    for axes in levels:
        ahead, value = level_scan(value, axes)
        aheads.append(ahead)
    entering = aheads[-1]
    for ahead in reversed(aheads[:-1]):
        entering = link(entering, ahead)
    return entering[1]


def attend_blocks(queries, own_keys, own_values, far_keys, far_values):
    score_scale = 1.0 / math.sqrt(P_SIZE)
    own_scores = (
        jnp.einsum("hbqd,hbkd->hbqk", queries, own_keys, preferred_element_type=f32) * score_scale
    )
    far_scores = (
        jnp.einsum("hbqd,hbkd->hbqk", queries, far_keys, preferred_element_type=f32) * score_scale
    )
    peak = jnp.maximum(
        jnp.max(own_scores, axis=-1, keepdims=True), jnp.max(far_scores, axis=-1, keepdims=True)
    )
    own_exp = jnp.exp(own_scores - peak)
    far_exp = jnp.exp(far_scores - peak)
    denominator = jnp.sum(own_exp, axis=-1, keepdims=True) + jnp.sum(
        far_exp, axis=-1, keepdims=True
    )
    own_weight = (own_exp / denominator).astype(bf16)
    far_weight = (far_exp / denominator).astype(bf16)
    mixed = jnp.einsum("hbqk,hbkd->hbqd", own_weight, own_values, preferred_element_type=f32)
    mixed = mixed + jnp.einsum(
        "hbqk,hbkd->hbqd", far_weight, far_values, preferred_element_type=f32
    )
    return mixed.astype(bf16)


def slot_ranks(owner_row, seq_count):
    owners_axis = jnp.arange(seq_count, dtype=jnp.int32)
    hits = (owner_row[:, None] == owners_axis[None, :]).astype(jnp.int32)
    return jnp.sum((jnp.cumsum(hits, axis=0) - hits) * hits, axis=1)


def per_device(
    tokens,
    norm_gain1,
    w_xz,
    w_bc,
    w_dt,
    dt_bias,
    decay_rate,
    curve_jump,
    skip_gain,
    norm_gain2,
    w_out,
    norm_gain3,
    w_q,
    w_kv,
    w_o,
    nbr_owner,
    nbr_block,
):
    token_count, width = tokens.shape
    seq_count = lax.axis_size(SEQ)
    block_count = token_count // BL
    request_count = block_count * KN
    slot_count = max(2, -(-request_count // seq_count))

    owner_flat = nbr_owner.reshape(-1)
    block_flat = nbr_block.reshape(-1)
    own_rank = slot_ranks(owner_flat, seq_count)
    targets = jnp.arange(seq_count, dtype=jnp.int32)[:, None, None]
    slots = jnp.arange(slot_count, dtype=jnp.int32)[None, :, None]
    match = (owner_flat[None, None, :] == targets) & (own_rank[None, None, :] == slots)
    wanted = jnp.sum(jnp.where(match, block_flat[None, None, :], 0), axis=2)
    send_index = lax.all_to_all(wanted, SEQ, split_axis=0, concat_axis=0, tiled=True)
    arrival_index = owner_flat * slot_count + own_rank

    normed1 = rms_rows(tokens, norm_gain1)
    x = heads_of(normed1, w_xz[:, :INNER])
    z = heads_of(normed1, w_xz[:, INNER:])
    maps = jnp.dot(normed1, w_bc, preferred_element_type=f32).astype(bf16)
    dt = jnp.einsum("td,dh->ht", normed1, w_dt, preferred_element_type=f32)
    u = jax.nn.softplus(dt + dt_bias[:, None])
    log_decay = -(decay_rate[:, None] * u + curve_jump[None, :])
    y_intra, prefix, before, local_state, local_total, running, cc = chunk_parts(
        x, maps[:, :NS], maps[:, NS:], u, log_decay
    )
    entering = device_prefix(local_total, local_state, (("y", "c"), ("x",), ("z",)))
    chunk_in = jnp.exp(before)[:, :, None, None] * entering[:, None] + prefix
    arriving = jnp.einsum("ctn,hcpn->hctp", cc.astype(f32), chunk_in, precision=highest)
    ssm = (y_intra + jnp.exp(running)[..., None] * arriving).reshape(H, token_count, P_SIZE)

    total = ssm + skip_gain[:, None, None] * x.astype(f32)
    gated = total * jax.nn.silu(z.astype(f32))
    head_normed = gated * lax.rsqrt(jnp.mean(gated * gated, axis=-1, keepdims=True) + epsilon)
    scaled = (head_normed * norm_gain2.reshape(H, 1, P_SIZE)).astype(bf16)
    middle = (
        tokens.astype(f32)
        + jnp.einsum(
            "htp,hpd->td", scaled, w_out.reshape(H, P_SIZE, width), preferred_element_type=f32
        )
    ).astype(bf16)

    normed = rms_rows(middle, norm_gain3)
    own_rows = normed.reshape(block_count, BL, width)
    outgoing = own_rows[send_index]
    arrived = lax.all_to_all(outgoing, SEQ, split_axis=0, concat_axis=0, tiled=True)
    far_rows = arrived.reshape(seq_count * slot_count, BL, width)[arrival_index]
    far_rows = far_rows.reshape(request_count * BL, width)

    queries = heads_of(normed, w_q).reshape(H, block_count, BL, P_SIZE)
    own_keys = heads_of(normed, w_kv[:, :INNER]).reshape(H, block_count, BL, P_SIZE)
    own_values = heads_of(normed, w_kv[:, INNER:]).reshape(H, block_count, BL, P_SIZE)
    far_keys = heads_of(far_rows, w_kv[:, :INNER]).reshape(H, block_count, KN * BL, P_SIZE)
    far_values = heads_of(far_rows, w_kv[:, INNER:]).reshape(H, block_count, KN * BL, P_SIZE)
    attended = attend_blocks(queries, own_keys, own_values, far_keys, far_values)
    attended = attended.reshape(H, token_count, P_SIZE)
    return (
        middle.astype(f32)
        + jnp.einsum(
            "hte,hed->td", attended, w_o.reshape(H, P_SIZE, width), preferred_element_type=f32
        )
    ).astype(bf16)


def solution(mesh):
    seq_shape = (mesh.shape["grp"], 4, mesh.shape["seq"] // 8, 2)
    fine = jax.sharding.Mesh(mesh.devices.reshape(seq_shape), CURVE)
    rows = P(CURVE, None)
    whole = P()
    in_specs = (rows, whole, whole, whole, whole, whole, whole, P(CURVE)) + (whole,) * 7 + (rows, rows)
    return jax.shard_map(
        per_device, mesh=fine, in_specs=in_specs, out_specs=rows, check_vma=False
    )
```

```python
import math

import jax
import jax.numpy as jnp
from jax import lax
from jax.sharding import PartitionSpec as P

H = 16
P_SIZE = 64
NS = 128
INNER = 1024
CH = 128
BL = 64
KN = 2


epsilon = 1e-05
highest = lax.Precision.HIGHEST
f32 = jnp.float32
bf16 = jnp.bfloat16
SEQ = ("x", "y", "c")
CURVE = ("z", "x", "y", "c")
def rms_rows(values, weights):
    floats = values.astype(f32)
    return (
        floats * lax.rsqrt(jnp.mean(floats * floats, axis=-1, keepdims=True) + epsilon) * weights
    ).astype(bf16)


def heads_of(rows, weight):
    flat = jnp.dot(rows, weight, preferred_element_type=f32).astype(bf16)
    return flat.reshape(rows.shape[0], H, P_SIZE).transpose(1, 0, 2)


def chunk_parts(x, b, c, u, log_decay):
    count = x.shape[1] // CH
    xc = x.reshape(H, count, CH, P_SIZE)
    bc = b.reshape(count, CH, NS)
    cc = c.reshape(count, CH, NS)
    uc = u.reshape(H, count, CH)
    running = jnp.cumsum(log_decay.reshape(H, count, CH), axis=2)
    lower = (jnp.arange(CH)[:, None] >= jnp.arange(CH)[None, :])[None, None]
    spread = running[..., :, None] - running[..., None, :]
    weights = jnp.where(lower, jnp.exp(jnp.where(lower, spread, 0.0)), 0.0)
    intersection = jnp.einsum("ctn,csn->cts", cc, bc, preferred_element_type=f32)
    mixing = (intersection[None] * weights * uc[:, :, None, :]).astype(bf16)
    y_intra = jnp.einsum("hcts,hcsp->hctp", mixing, xc, preferred_element_type=f32)
    last = running[..., -1]
    tail_weight = jnp.exp(last[..., None] - running) * uc
    tail = (tail_weight[..., None] * xc.astype(f32)).astype(bf16)
    chunk_state = jnp.einsum("hcsp,csn->hcpn", tail, bc, preferred_element_type=f32)
    prefix = [jnp.zeros((H, P_SIZE, NS), f32)]
    before = [jnp.zeros((H,), f32)]
    for k in range(count):
        prefix.append(jnp.exp(last[:, k])[:, None, None] * prefix[-1] + chunk_state[:, k])
        before.append(before[-1] + last[:, k])
    return (
        y_intra,
        jnp.stack(prefix[:count], axis=1),
        jnp.stack(before[:count], axis=1),
        prefix[count],
        before[count],
        running,
        cc,
    )


def to_wire(total, state):
    high = total.astype(bf16)
    rest = total - high.astype(f32)
    middle = rest.astype(bf16)
    low = (rest - middle.astype(f32)).astype(bf16)
    pieces = jnp.pad(jnp.stack([high, middle, low]), ((0, 5), (0, NS - H)))
    return jnp.concatenate([state.reshape(H * P_SIZE, NS).astype(bf16), pieces], axis=0)


def from_wire(wire):
    pieces = wire[H * P_SIZE : H * P_SIZE + 3, :H].astype(f32)
    total = pieces[0] + pieces[1] + pieces[2]
    return total, wire[: H * P_SIZE].astype(f32).reshape(H, P_SIZE, NS)


def link(earlier, later):
    return (earlier[0] + later[0], jnp.exp(later[0])[:, None, None] * earlier[1] + later[1])


def level_scan(value, axes):
    members = lax.axis_size(axes)
    place = lax.axis_index(axes)
    wire = to_wire(*value)
    copies = jnp.broadcast_to(wire[None], (members,) + wire.shape)
    everyone = lax.all_to_all(copies, axes, split_axis=0, concat_axis=0, tiled=True)
    totals = jnp.sum(everyone[:, H * P_SIZE : H * P_SIZE + 3, :H].astype(f32), axis=1)
    states = everyone[:, : H * P_SIZE].reshape(members, H, P_SIZE, NS)
    order = jnp.arange(members)
    later = order[None, :] > order[:, None]
    before_me = order < place
    ahead_span = jnp.sum(jnp.where((later & before_me[None, :])[..., None], totals[None], 0.0), axis=1)
    whole_span = jnp.sum(jnp.where(later[..., None], totals[None], 0.0), axis=1)
    ahead_weight = jnp.where(before_me[:, None], jnp.exp(ahead_span), 0.0)
    whole_weight = jnp.exp(whole_span)
    ahead = (
        jnp.sum(jnp.where(before_me[:, None], totals, 0.0), axis=0),
        jnp.sum(ahead_weight[:, :, None, None] * states.astype(f32), axis=0),
    )
    whole = (
        jnp.sum(totals, axis=0),
        jnp.sum(whole_weight[:, :, None, None] * states.astype(f32), axis=0),
    )
    return ahead, whole


def device_prefix(total, state, levels):
    value = (total, state)
    aheads = []
    for axes in levels:
        ahead, value = level_scan(value, axes)
        aheads.append(ahead)
    entering = aheads[-1]
    for ahead in reversed(aheads[:-1]):
        entering = link(entering, ahead)
    return entering[1]


def attend_blocks(queries, own_keys, own_values, far_keys, far_values):
    score_scale = 1.0 / math.sqrt(P_SIZE)
    own_scores = (
        jnp.einsum("hbqd,hbkd->hbqk", queries, own_keys, preferred_element_type=f32) * score_scale
    )
    far_scores = (
        jnp.einsum("hbqd,hbkd->hbqk", queries, far_keys, preferred_element_type=f32) * score_scale
    )
    peak = jnp.maximum(
        jnp.max(own_scores, axis=-1, keepdims=True), jnp.max(far_scores, axis=-1, keepdims=True)
    )
    own_exp = jnp.exp(own_scores - peak)
    far_exp = jnp.exp(far_scores - peak)
    denominator = jnp.sum(own_exp, axis=-1, keepdims=True) + jnp.sum(
        far_exp, axis=-1, keepdims=True
    )
    own_weight = (own_exp / denominator).astype(bf16)
    far_weight = (far_exp / denominator).astype(bf16)
    mixed = jnp.einsum("hbqk,hbkd->hbqd", own_weight, own_values, preferred_element_type=f32)
    mixed = mixed + jnp.einsum(
        "hbqk,hbkd->hbqd", far_weight, far_values, preferred_element_type=f32
    )
    return mixed.astype(bf16)


def slot_ranks(owner_row, seq_count):
    owners_axis = jnp.arange(seq_count, dtype=jnp.int32)
    hits = (owner_row[:, None] == owners_axis[None, :]).astype(jnp.int32)
    return jnp.sum((jnp.cumsum(hits, axis=0) - hits) * hits, axis=1)


def per_device(
    tokens,
    norm_gain1,
    w_xz,
    w_bc,
    w_dt,
    dt_bias,
    decay_rate,
    curve_jump,
    skip_gain,
    norm_gain2,
    w_out,
    norm_gain3,
    w_q,
    w_kv,
    w_o,
    nbr_owner,
    nbr_block,
):
    token_count, width = tokens.shape
    seq_count = lax.axis_size(SEQ)
    block_count = token_count // BL
    request_count = block_count * KN
    slot_count = max(2, -(-request_count // seq_count))

    owner_flat = nbr_owner.reshape(-1)
    block_flat = nbr_block.reshape(-1)
    own_rank = slot_ranks(owner_flat, seq_count)
    targets = jnp.arange(seq_count, dtype=jnp.int32)[:, None, None]
    slots = jnp.arange(slot_count, dtype=jnp.int32)[None, :, None]
    match = (owner_flat[None, None, :] == targets) & (own_rank[None, None, :] == slots)
    wanted = jnp.sum(jnp.where(match, block_flat[None, None, :], 0), axis=2)
    send_index = lax.all_to_all(wanted, SEQ, split_axis=0, concat_axis=0, tiled=True)
    arrival_index = owner_flat * slot_count + own_rank

    normed1 = rms_rows(tokens, norm_gain1)
    x = heads_of(normed1, w_xz[:, :INNER])
    z = heads_of(normed1, w_xz[:, INNER:])
    maps = jnp.dot(normed1, w_bc, preferred_element_type=f32).astype(bf16)
    dt = jnp.einsum("td,dh->ht", normed1, w_dt, preferred_element_type=f32)
    u = jax.nn.softplus(dt + dt_bias[:, None])
    log_decay = -(decay_rate[:, None] * u + curve_jump[None, :])
    y_intra, prefix, before, local_state, local_total, running, cc = chunk_parts(
        x, maps[:, :NS], maps[:, NS:], u, log_decay
    )
    entering = device_prefix(local_total, local_state, (("y", "c"), ("x",), ("z",)))
    chunk_in = jnp.exp(before)[:, :, None, None] * entering[:, None] + prefix
    arriving = jnp.einsum("ctn,hcpn->hctp", cc.astype(f32), chunk_in, precision=highest)
    ssm = (y_intra + jnp.exp(running)[..., None] * arriving).reshape(H, token_count, P_SIZE)

    total = ssm + skip_gain[:, None, None] * x.astype(f32)
    gated = total * jax.nn.silu(z.astype(f32))
    head_normed = gated * lax.rsqrt(jnp.mean(gated * gated, axis=-1, keepdims=True) + epsilon)
    scaled = (head_normed * norm_gain2.reshape(H, 1, P_SIZE)).astype(bf16)
    middle = (
        tokens.astype(f32)
        + jnp.einsum(
            "htp,hpd->td", scaled, w_out.reshape(H, P_SIZE, width), preferred_element_type=f32
        )
    ).astype(bf16)

    normed = rms_rows(middle, norm_gain3)
    own_rows = normed.reshape(block_count, BL, width)
    outgoing = own_rows[send_index]
    arrived = lax.all_to_all(outgoing, SEQ, split_axis=0, concat_axis=0, tiled=True)
    far_rows = arrived.reshape(seq_count * slot_count, BL, width)[arrival_index]
    far_rows = far_rows.reshape(request_count * BL, width)

    queries = heads_of(normed, w_q).reshape(H, block_count, BL, P_SIZE)
    own_keys = heads_of(normed, w_kv[:, :INNER]).reshape(H, block_count, BL, P_SIZE)
    own_values = heads_of(normed, w_kv[:, INNER:]).reshape(H, block_count, BL, P_SIZE)
    far_keys = heads_of(far_rows, w_kv[:, :INNER]).reshape(H, block_count, KN * BL, P_SIZE)
    far_values = heads_of(far_rows, w_kv[:, INNER:]).reshape(H, block_count, KN * BL, P_SIZE)
    attended = attend_blocks(queries, own_keys, own_values, far_keys, far_values)
    attended = attended.reshape(H, token_count, P_SIZE)
    return (
        middle.astype(f32)
        + jnp.einsum(
            "hte,hed->td", attended, w_o.reshape(H, P_SIZE, width), preferred_element_type=f32
        )
    ).astype(bf16)


def solution(mesh):
    seq_shape = (mesh.shape["grp"], 4, mesh.shape["seq"] // 8, 2)
    fine = jax.sharding.Mesh(mesh.devices.reshape(seq_shape), CURVE)
    rows = P(CURVE, None)
    whole = P()
    in_specs = (rows, whole, whole, whole, whole, whole, whole, P(CURVE)) + (whole,) * 7 + (rows, rows)
    return jax.shard_map(
        per_device, mesh=fine, in_specs=in_specs, out_specs=rows, check_vma=False
    )
```

```python
import math

import jax
import jax.numpy as jnp
from jax import lax
from jax.sharding import PartitionSpec as P

H = 16
P_SIZE = 64
NS = 128
INNER = 1024
CH = 128
BL = 64
KN = 2


epsilon = 1e-05
highest = lax.Precision.HIGHEST
f32 = jnp.float32
bf16 = jnp.bfloat16
SEQ = ("x", "y", "c")
CURVE = ("z", "x", "y", "c")
def rms_rows(values, weights):
    floats = values.astype(f32)
    return (
        floats * lax.rsqrt(jnp.mean(floats * floats, axis=-1, keepdims=True) + epsilon) * weights
    ).astype(bf16)


def heads_of(rows, weight):
    flat = jnp.dot(rows, weight, preferred_element_type=f32).astype(bf16)
    return flat.reshape(rows.shape[0], H, P_SIZE).transpose(1, 0, 2)


def chunk_parts(x, b, c, u, log_decay):
    count = x.shape[1] // CH
    xc = x.reshape(H, count, CH, P_SIZE)
    bc = b.reshape(count, CH, NS)
    cc = c.reshape(count, CH, NS)
    uc = u.reshape(H, count, CH)
    running = jnp.cumsum(log_decay.reshape(H, count, CH), axis=2)
    lower = (jnp.arange(CH)[:, None] >= jnp.arange(CH)[None, :])[None, None]
    spread = running[..., :, None] - running[..., None, :]
    weights = jnp.where(lower, jnp.exp(jnp.where(lower, spread, 0.0)), 0.0)
    intersection = jnp.einsum("ctn,csn->cts", cc, bc, preferred_element_type=f32)
    mixing = (intersection[None] * weights * uc[:, :, None, :]).astype(bf16)
    y_intra = jnp.einsum("hcts,hcsp->hctp", mixing, xc, preferred_element_type=f32)
    last = running[..., -1]
    tail_weight = jnp.exp(last[..., None] - running) * uc
    tail = (tail_weight[..., None] * xc.astype(f32)).astype(bf16)
    chunk_state = jnp.einsum("hcsp,csn->hcpn", tail, bc, preferred_element_type=f32)
    prefix = [jnp.zeros((H, P_SIZE, NS), f32)]
    before = [jnp.zeros((H,), f32)]
    for k in range(count):
        prefix.append(jnp.exp(last[:, k])[:, None, None] * prefix[-1] + chunk_state[:, k])
        before.append(before[-1] + last[:, k])
    return (
        y_intra,
        jnp.stack(prefix[:count], axis=1),
        jnp.stack(before[:count], axis=1),
        prefix[count],
        before[count],
        running,
        cc,
    )


def to_wire(total, state, notes):
    high = total.astype(bf16)
    rest = total - high.astype(f32)
    middle = rest.astype(bf16)
    low = (rest - middle.astype(f32)).astype(bf16)
    members = notes.shape[0]
    pieces = jnp.pad(jnp.stack([high, middle, low]), ((0, 0), (0, NS - H)))
    pieces = jnp.broadcast_to(pieces[None], (members, 3, NS))
    notes = jnp.pad(notes.astype(bf16), ((0, 0), (0, NS - notes.shape[1])))[:, None]
    tail = jnp.concatenate([pieces, notes, jnp.zeros((members, 4, NS), bf16)], axis=1)
    body = state.reshape(H * P_SIZE, NS).astype(bf16)
    return jnp.concatenate([jnp.broadcast_to(body[None], (members,) + body.shape), tail], axis=1)


def link(earlier, later):
    return (earlier[0] + later[0], jnp.exp(later[0])[:, None, None] * earlier[1] + later[1])


def level_scan(value, axes, notes):
    members = lax.axis_size(axes)
    place = lax.axis_index(axes)
    copies = to_wire(value[0], value[1], notes)
    everyone = lax.all_to_all(copies, axes, split_axis=0, concat_axis=0, tiled=True)
    totals = jnp.sum(everyone[:, H * P_SIZE : H * P_SIZE + 3, :H].astype(f32), axis=1)
    heard = everyone[:, H * P_SIZE + 3, : notes.shape[1]]
    states = everyone[:, : H * P_SIZE].reshape(members, H, P_SIZE, NS)
    order = jnp.arange(members)
    later = order[None, :] > order[:, None]
    before_me = order < place
    ahead_span = jnp.sum(jnp.where((later & before_me[None, :])[..., None], totals[None], 0.0), axis=1)
    whole_span = jnp.sum(jnp.where(later[..., None], totals[None], 0.0), axis=1)
    ahead_weight = jnp.where(before_me[:, None], jnp.exp(ahead_span), 0.0)
    whole_weight = jnp.exp(whole_span)
    ahead = (
        jnp.sum(jnp.where(before_me[:, None], totals, 0.0), axis=0),
        jnp.sum(ahead_weight[:, :, None, None] * states.astype(f32), axis=0),
    )
    whole = (
        jnp.sum(totals, axis=0),
        jnp.sum(whole_weight[:, :, None, None] * states.astype(f32), axis=0),
    )
    return ahead, whole, heard


def device_prefix(total, state, wanted):
    cores = lax.axis_size(("y", "c"))
    rows = lax.axis_size("x")
    by_column = wanted.reshape(rows, cores, -1).transpose(1, 0, 2).reshape(cores, -1)
    first, value, heard = level_scan((total, state), ("y", "c"), by_column)
    slot_count = wanted.shape[1]
    by_row = heard.reshape(cores, rows, slot_count).transpose(1, 0, 2).reshape(rows, -1)
    second, value, heard = level_scan(value, ("x",), by_row)
    send_index = heard.reshape(rows * cores, slot_count).astype(jnp.int32)
    third, value, _ = level_scan(value, ("z",), jnp.zeros((lax.axis_size("z"), 1), bf16))
    entering = link(link(third, second), first)
    return entering[1], send_index


def attend_blocks(queries, own_keys, own_values, far_keys, far_values):
    score_scale = 1.0 / math.sqrt(P_SIZE)
    own_scores = (
        jnp.einsum("hbqd,hbkd->hbqk", queries, own_keys, preferred_element_type=f32) * score_scale
    )
    far_scores = (
        jnp.einsum("hbqd,hbkd->hbqk", queries, far_keys, preferred_element_type=f32) * score_scale
    )
    peak = jnp.maximum(
        jnp.max(own_scores, axis=-1, keepdims=True), jnp.max(far_scores, axis=-1, keepdims=True)
    )
    own_exp = jnp.exp(own_scores - peak)
    far_exp = jnp.exp(far_scores - peak)
    denominator = jnp.sum(own_exp, axis=-1, keepdims=True) + jnp.sum(
        far_exp, axis=-1, keepdims=True
    )
    own_weight = (own_exp / denominator).astype(bf16)
    far_weight = (far_exp / denominator).astype(bf16)
    mixed = jnp.einsum("hbqk,hbkd->hbqd", own_weight, own_values, preferred_element_type=f32)
    mixed = mixed + jnp.einsum(
        "hbqk,hbkd->hbqd", far_weight, far_values, preferred_element_type=f32
    )
    return mixed.astype(bf16)


def slot_ranks(owner_row, seq_count):
    owners_axis = jnp.arange(seq_count, dtype=jnp.int32)
    hits = (owner_row[:, None] == owners_axis[None, :]).astype(jnp.int32)
    return jnp.sum((jnp.cumsum(hits, axis=0) - hits) * hits, axis=1)


def per_device(
    tokens,
    norm_gain1,
    w_xz,
    w_bc,
    w_dt,
    dt_bias,
    decay_rate,
    curve_jump,
    skip_gain,
    norm_gain2,
    w_out,
    norm_gain3,
    w_q,
    w_kv,
    w_o,
    nbr_owner,
    nbr_block,
):
    token_count, width = tokens.shape
    seq_count = lax.axis_size(SEQ)
    block_count = token_count // BL
    request_count = block_count * KN
    slot_count = max(2, -(-request_count // seq_count))

    owner_flat = nbr_owner.reshape(-1)
    block_flat = nbr_block.reshape(-1)
    own_rank = slot_ranks(owner_flat, seq_count)
    targets = jnp.arange(seq_count, dtype=jnp.int32)[:, None, None]
    slots = jnp.arange(slot_count, dtype=jnp.int32)[None, :, None]
    match = (owner_flat[None, None, :] == targets) & (own_rank[None, None, :] == slots)
    wanted = jnp.sum(jnp.where(match, block_flat[None, None, :], 0), axis=2)
    arrival_index = owner_flat * slot_count + own_rank

    normed1 = rms_rows(tokens, norm_gain1)
    x = heads_of(normed1, w_xz[:, :INNER])
    z = heads_of(normed1, w_xz[:, INNER:])
    maps = jnp.dot(normed1, w_bc, preferred_element_type=f32).astype(bf16)
    dt = jnp.einsum("td,dh->ht", normed1, w_dt, preferred_element_type=f32)
    u = jax.nn.softplus(dt + dt_bias[:, None])
    log_decay = -(decay_rate[:, None] * u + curve_jump[None, :])
    y_intra, prefix, before, local_state, local_total, running, cc = chunk_parts(
        x, maps[:, :NS], maps[:, NS:], u, log_decay
    )
    entering, send_index = device_prefix(local_total, local_state, wanted)
    chunk_in = jnp.exp(before)[:, :, None, None] * entering[:, None] + prefix
    arriving = jnp.einsum("ctn,hcpn->hctp", cc.astype(f32), chunk_in, precision=highest)
    ssm = (y_intra + jnp.exp(running)[..., None] * arriving).reshape(H, token_count, P_SIZE)

    total = ssm + skip_gain[:, None, None] * x.astype(f32)
    gated = total * jax.nn.silu(z.astype(f32))
    head_normed = gated * lax.rsqrt(jnp.mean(gated * gated, axis=-1, keepdims=True) + epsilon)
    scaled = (head_normed * norm_gain2.reshape(H, 1, P_SIZE)).astype(bf16)
    middle = (
        tokens.astype(f32)
        + jnp.einsum(
            "htp,hpd->td", scaled, w_out.reshape(H, P_SIZE, width), preferred_element_type=f32
        )
    ).astype(bf16)

    normed = rms_rows(middle, norm_gain3)
    own_rows = normed.reshape(block_count, BL, width)
    outgoing = own_rows[send_index]
    arrived = lax.all_to_all(outgoing, SEQ, split_axis=0, concat_axis=0, tiled=True)
    far_rows = arrived.reshape(seq_count * slot_count, BL, width)[arrival_index]
    far_rows = far_rows.reshape(request_count * BL, width)

    queries = heads_of(normed, w_q).reshape(H, block_count, BL, P_SIZE)
    own_keys = heads_of(normed, w_kv[:, :INNER]).reshape(H, block_count, BL, P_SIZE)
    own_values = heads_of(normed, w_kv[:, INNER:]).reshape(H, block_count, BL, P_SIZE)
    far_keys = heads_of(far_rows, w_kv[:, :INNER]).reshape(H, block_count, KN * BL, P_SIZE)
    far_values = heads_of(far_rows, w_kv[:, INNER:]).reshape(H, block_count, KN * BL, P_SIZE)
    attended = attend_blocks(queries, own_keys, own_values, far_keys, far_values)
    attended = attended.reshape(H, token_count, P_SIZE)
    return (
        middle.astype(f32)
        + jnp.einsum(
            "hte,hed->td", attended, w_o.reshape(H, P_SIZE, width), preferred_element_type=f32
        )
    ).astype(bf16)


def solution(mesh):
    seq_shape = (mesh.shape["grp"], 4, mesh.shape["seq"] // 8, 2)
    fine = jax.sharding.Mesh(mesh.devices.reshape(seq_shape), CURVE)
    rows = P(CURVE, None)
    whole = P()
    in_specs = (rows, whole, whole, whole, whole, whole, whole, P(CURVE)) + (whole,) * 7 + (rows, rows)
    return jax.shard_map(
        per_device, mesh=fine, in_specs=in_specs, out_specs=rows, check_vma=False
    )
```

```python
import math

import jax
import jax.numpy as jnp
from jax import lax
from jax.sharding import PartitionSpec as P

H = 16
P_SIZE = 64
NS = 128
INNER = 1024
CH = 128
BL = 64
KN = 2


epsilon = 1e-05
highest = lax.Precision.HIGHEST
f32 = jnp.float32
bf16 = jnp.bfloat16
SEQ = ("x", "y", "c")
CURVE = ("z", "x", "y", "c")
def rms_rows(values, weights):
    floats = values.astype(f32)
    return (
        floats * lax.rsqrt(jnp.mean(floats * floats, axis=-1, keepdims=True) + epsilon) * weights
    ).astype(bf16)


def heads_of(rows, weight):
    flat = jnp.dot(rows, weight, preferred_element_type=f32).astype(bf16)
    return flat.reshape(rows.shape[0], H, P_SIZE).transpose(1, 0, 2)


def chunk_parts(x, b, c, u, log_decay):
    count = x.shape[1] // CH
    xc = x.reshape(H, count, CH, P_SIZE)
    bc = b.reshape(count, CH, NS)
    cc = c.reshape(count, CH, NS)
    uc = u.reshape(H, count, CH)
    running = jnp.cumsum(log_decay.reshape(H, count, CH), axis=2)
    lower = (jnp.arange(CH)[:, None] >= jnp.arange(CH)[None, :])[None, None]
    spread = running[..., :, None] - running[..., None, :]
    weights = jnp.where(lower, jnp.exp(jnp.where(lower, spread, 0.0)), 0.0)
    intersection = jnp.einsum("ctn,csn->cts", cc, bc, preferred_element_type=f32)
    mixing = (intersection[None] * weights * uc[:, :, None, :]).astype(bf16)
    y_intra = jnp.einsum("hcts,hcsp->hctp", mixing, xc, preferred_element_type=f32)
    last = running[..., -1]
    tail_weight = jnp.exp(last[..., None] - running) * uc
    tail = (tail_weight[..., None] * xc.astype(f32)).astype(bf16)
    chunk_state = jnp.einsum("hcsp,csn->hcpn", tail, bc, preferred_element_type=f32)
    prefix = [jnp.zeros((H, P_SIZE, NS), f32)]
    before = [jnp.zeros((H,), f32)]
    for k in range(count):
        prefix.append(jnp.exp(last[:, k])[:, None, None] * prefix[-1] + chunk_state[:, k])
        before.append(before[-1] + last[:, k])
    return (
        y_intra,
        jnp.stack(prefix[:count], axis=1),
        jnp.stack(before[:count], axis=1),
        prefix[count],
        before[count],
        running,
        cc,
    )


def to_wire(total, state, notes):
    high = total.astype(bf16)
    rest = total - high.astype(f32)
    middle = rest.astype(bf16)
    low = (rest - middle.astype(f32)).astype(bf16)
    pieces = jnp.pad(jnp.stack([high, middle, low]), ((0, 5), (0, NS - H)))
    wire = jnp.concatenate([state.reshape(H * P_SIZE, NS).astype(bf16), pieces], axis=0)
    notes = jnp.pad(notes.astype(bf16), ((0, 0), (0, NS - notes.shape[1])))
    row = lax.broadcasted_iota(jnp.int32, (1, wire.shape[0], 1), 1)
    return jnp.where(row == H * P_SIZE + 3, notes[:, None, :], wire[None])


def link(earlier, later):
    return (earlier[0] + later[0], jnp.exp(later[0])[:, None, None] * earlier[1] + later[1])


def level_scan(value, axes, notes):
    members = lax.axis_size(axes)
    place = lax.axis_index(axes)
    copies = to_wire(value[0], value[1], notes)
    everyone = lax.all_to_all(copies, axes, split_axis=0, concat_axis=0, tiled=True)
    totals = jnp.sum(everyone[:, H * P_SIZE : H * P_SIZE + 3, :H].astype(f32), axis=1)
    heard = everyone[:, H * P_SIZE + 3, : notes.shape[1]]
    states = everyone[:, : H * P_SIZE].reshape(members, H, P_SIZE, NS)
    order = jnp.arange(members)
    later = order[None, :] > order[:, None]
    before_me = order < place
    ahead_span = jnp.sum(jnp.where((later & before_me[None, :])[..., None], totals[None], 0.0), axis=1)
    whole_span = jnp.sum(jnp.where(later[..., None], totals[None], 0.0), axis=1)
    ahead_weight = jnp.where(before_me[:, None], jnp.exp(ahead_span), 0.0)
    whole_weight = jnp.exp(whole_span)
    ahead = (
        jnp.sum(jnp.where(before_me[:, None], totals, 0.0), axis=0),
        jnp.sum(ahead_weight[:, :, None, None] * states.astype(f32), axis=0),
    )
    whole = (
        jnp.sum(totals, axis=0),
        jnp.sum(whole_weight[:, :, None, None] * states.astype(f32), axis=0),
    )
    return ahead, whole, heard


def device_prefix(total, state, wanted):
    cores = lax.axis_size(("y", "c"))
    rows = lax.axis_size("x")
    by_column = wanted.reshape(rows, cores, -1).transpose(1, 0, 2).reshape(cores, -1)
    first, value, heard = level_scan((total, state), ("y", "c"), by_column)
    slot_count = wanted.shape[1]
    by_row = heard.reshape(cores, rows, slot_count).transpose(1, 0, 2).reshape(rows, -1)
    second, value, heard = level_scan(value, ("x",), by_row)
    send_index = heard.reshape(rows * cores, slot_count).astype(jnp.int32)
    third, value, _ = level_scan(value, ("z",), jnp.zeros((lax.axis_size("z"), 1), bf16))
    entering = link(link(third, second), first)
    return entering[1], send_index


def attend_blocks(queries, own_keys, own_values, far_keys, far_values):
    score_scale = 1.0 / math.sqrt(P_SIZE)
    own_scores = (
        jnp.einsum("hbqd,hbkd->hbqk", queries, own_keys, preferred_element_type=f32) * score_scale
    )
    far_scores = (
        jnp.einsum("hbqd,hbkd->hbqk", queries, far_keys, preferred_element_type=f32) * score_scale
    )
    peak = jnp.maximum(
        jnp.max(own_scores, axis=-1, keepdims=True), jnp.max(far_scores, axis=-1, keepdims=True)
    )
    own_exp = jnp.exp(own_scores - peak)
    far_exp = jnp.exp(far_scores - peak)
    denominator = jnp.sum(own_exp, axis=-1, keepdims=True) + jnp.sum(
        far_exp, axis=-1, keepdims=True
    )
    own_weight = (own_exp / denominator).astype(bf16)
    far_weight = (far_exp / denominator).astype(bf16)
    mixed = jnp.einsum("hbqk,hbkd->hbqd", own_weight, own_values, preferred_element_type=f32)
    mixed = mixed + jnp.einsum(
        "hbqk,hbkd->hbqd", far_weight, far_values, preferred_element_type=f32
    )
    return mixed.astype(bf16)


def slot_ranks(owner_row, seq_count):
    owners_axis = jnp.arange(seq_count, dtype=jnp.int32)
    hits = (owner_row[:, None] == owners_axis[None, :]).astype(jnp.int32)
    return jnp.sum((jnp.cumsum(hits, axis=0) - hits) * hits, axis=1)


def per_device(
    tokens,
    norm_gain1,
    w_xz,
    w_bc,
    w_dt,
    dt_bias,
    decay_rate,
    curve_jump,
    skip_gain,
    norm_gain2,
    w_out,
    norm_gain3,
    w_q,
    w_kv,
    w_o,
    nbr_owner,
    nbr_block,
):
    token_count, width = tokens.shape
    seq_count = lax.axis_size(SEQ)
    block_count = token_count // BL
    request_count = block_count * KN
    slot_count = max(2, -(-request_count // seq_count))

    owner_flat = nbr_owner.reshape(-1)
    block_flat = nbr_block.reshape(-1)
    own_rank = slot_ranks(owner_flat, seq_count)
    targets = jnp.arange(seq_count, dtype=jnp.int32)[:, None, None]
    slots = jnp.arange(slot_count, dtype=jnp.int32)[None, :, None]
    match = (owner_flat[None, None, :] == targets) & (own_rank[None, None, :] == slots)
    wanted = jnp.sum(jnp.where(match, block_flat[None, None, :], 0), axis=2)
    arrival_index = owner_flat * slot_count + own_rank

    normed1 = rms_rows(tokens, norm_gain1)
    x = heads_of(normed1, w_xz[:, :INNER])
    z = heads_of(normed1, w_xz[:, INNER:])
    maps = jnp.dot(normed1, w_bc, preferred_element_type=f32).astype(bf16)
    dt = jnp.einsum("td,dh->ht", normed1, w_dt, preferred_element_type=f32)
    u = jax.nn.softplus(dt + dt_bias[:, None])
    log_decay = -(decay_rate[:, None] * u + curve_jump[None, :])
    y_intra, prefix, before, local_state, local_total, running, cc = chunk_parts(
        x, maps[:, :NS], maps[:, NS:], u, log_decay
    )
    entering, send_index = device_prefix(local_total, local_state, wanted)
    chunk_in = jnp.exp(before)[:, :, None, None] * entering[:, None] + prefix
    arriving = jnp.einsum("ctn,hcpn->hctp", cc.astype(f32), chunk_in, precision=highest)
    ssm = (y_intra + jnp.exp(running)[..., None] * arriving).reshape(H, token_count, P_SIZE)

    total = ssm + skip_gain[:, None, None] * x.astype(f32)
    gated = total * jax.nn.silu(z.astype(f32))
    head_normed = gated * lax.rsqrt(jnp.mean(gated * gated, axis=-1, keepdims=True) + epsilon)
    scaled = (head_normed * norm_gain2.reshape(H, 1, P_SIZE)).astype(bf16)
    middle = (
        tokens.astype(f32)
        + jnp.einsum(
            "htp,hpd->td", scaled, w_out.reshape(H, P_SIZE, width), preferred_element_type=f32
        )
    ).astype(bf16)

    normed = rms_rows(middle, norm_gain3)
    own_rows = normed.reshape(block_count, BL, width)
    outgoing = own_rows[send_index]
    arrived = lax.all_to_all(outgoing, SEQ, split_axis=0, concat_axis=0, tiled=True)
    far_rows = arrived.reshape(seq_count * slot_count, BL, width)[arrival_index]
    far_rows = far_rows.reshape(request_count * BL, width)

    queries = heads_of(normed, w_q).reshape(H, block_count, BL, P_SIZE)
    own_keys = heads_of(normed, w_kv[:, :INNER]).reshape(H, block_count, BL, P_SIZE)
    own_values = heads_of(normed, w_kv[:, INNER:]).reshape(H, block_count, BL, P_SIZE)
    far_keys = heads_of(far_rows, w_kv[:, :INNER]).reshape(H, block_count, KN * BL, P_SIZE)
    far_values = heads_of(far_rows, w_kv[:, INNER:]).reshape(H, block_count, KN * BL, P_SIZE)
    attended = attend_blocks(queries, own_keys, own_values, far_keys, far_values)
    attended = attended.reshape(H, token_count, P_SIZE)
    return (
        middle.astype(f32)
        + jnp.einsum(
            "hte,hed->td", attended, w_o.reshape(H, P_SIZE, width), preferred_element_type=f32
        )
    ).astype(bf16)


def solution(mesh):
    seq_shape = (mesh.shape["grp"], 4, mesh.shape["seq"] // 8, 2)
    fine = jax.sharding.Mesh(mesh.devices.reshape(seq_shape), CURVE)
    rows = P(CURVE, None)
    whole = P()
    in_specs = (rows, whole, whole, whole, whole, whole, whole, P(CURVE)) + (whole,) * 7 + (rows, rows)
    return jax.shard_map(
        per_device, mesh=fine, in_specs=in_specs, out_specs=rows, check_vma=False
    )
```

```python
import math

import jax
import jax.numpy as jnp
from jax import lax
from jax.sharding import PartitionSpec as P

H = 16
P_SIZE = 64
NS = 128
INNER = 1024
CH = 128
BL = 64
KN = 2


epsilon = 1e-05
highest = lax.Precision.HIGHEST
f32 = jnp.float32
bf16 = jnp.bfloat16
SEQ = ("x", "y", "c")
CURVE = ("z", "x", "y", "c")
def rms_rows(values, weights):
    floats = values.astype(f32)
    return (
        floats * lax.rsqrt(jnp.mean(floats * floats, axis=-1, keepdims=True) + epsilon) * weights
    ).astype(bf16)


def heads_of(rows, weight):
    flat = jnp.dot(rows, weight, preferred_element_type=f32).astype(bf16)
    return flat.reshape(rows.shape[0], H, P_SIZE).transpose(1, 0, 2)


def chunk_parts(x, b, c, u, log_decay):
    count = x.shape[1] // CH
    xc = x.reshape(H, count, CH, P_SIZE)
    bc = b.reshape(count, CH, NS)
    cc = c.reshape(count, CH, NS)
    uc = u.reshape(H, count, CH)
    running = jnp.cumsum(log_decay.reshape(H, count, CH), axis=2)
    lower = (jnp.arange(CH)[:, None] >= jnp.arange(CH)[None, :])[None, None]
    spread = running[..., :, None] - running[..., None, :]
    weights = jnp.where(lower, jnp.exp(jnp.where(lower, spread, 0.0)), 0.0)
    intersection = jnp.einsum("ctn,csn->cts", cc, bc, preferred_element_type=f32)
    mixing = (intersection[None] * weights * uc[:, :, None, :]).astype(bf16)
    y_intra = jnp.einsum("hcts,hcsp->hctp", mixing, xc, preferred_element_type=f32)
    last = running[..., -1]
    tail_weight = jnp.exp(last[..., None] - running) * uc
    tail = (tail_weight[..., None] * xc.astype(f32)).astype(bf16)
    chunk_state = jnp.einsum("hcsp,csn->hcpn", tail, bc, preferred_element_type=f32)
    prefix = [jnp.zeros((H, P_SIZE, NS), f32)]
    before = [jnp.zeros((H,), f32)]
    for k in range(count):
        prefix.append(jnp.exp(last[:, k])[:, None, None] * prefix[-1] + chunk_state[:, k])
        before.append(before[-1] + last[:, k])
    return (
        y_intra,
        jnp.stack(prefix[:count], axis=1),
        jnp.stack(before[:count], axis=1),
        prefix[count],
        before[count],
        running,
        cc,
    )


def to_wire(total, state):
    high = total.astype(bf16)
    rest = total - high.astype(f32)
    middle = rest.astype(bf16)
    low = (rest - middle.astype(f32)).astype(bf16)
    pieces = jnp.pad(jnp.stack([high, middle, low]), ((0, 5), (0, NS - H)))
    return jnp.concatenate([state.reshape(H * P_SIZE, NS).astype(bf16), pieces], axis=0)


def from_wire(wire):
    pieces = wire[H * P_SIZE : H * P_SIZE + 3, :H].astype(f32)
    total = pieces[0] + pieces[1] + pieces[2]
    return total, wire[: H * P_SIZE].astype(f32).reshape(H, P_SIZE, NS)


def link(earlier, later):
    return (earlier[0] + later[0], jnp.exp(later[0])[:, None, None] * earlier[1] + later[1])


def level_scan(value, axes, rider=None):
    members = lax.axis_size(axes)
    place = lax.axis_index(axes)
    wire = to_wire(*value)
    copies = jnp.broadcast_to(wire[None], (members,) + wire.shape)
    if rider is not None:
        copies, rider = lax.optimization_barrier((copies, rider))
    everyone = lax.all_to_all(copies, axes, split_axis=0, concat_axis=0, tiled=True)
    if rider is not None:
        rider = lax.all_to_all(rider, SEQ, split_axis=0, concat_axis=0, tiled=True)
        everyone, rider = lax.optimization_barrier((everyone, rider))
    totals = jnp.sum(everyone[:, H * P_SIZE : H * P_SIZE + 3, :H].astype(f32), axis=1)
    states = everyone[:, : H * P_SIZE].reshape(members, H, P_SIZE, NS)
    order = jnp.arange(members)
    later = order[None, :] > order[:, None]
    before_me = order < place
    ahead_span = jnp.sum(jnp.where((later & before_me[None, :])[..., None], totals[None], 0.0), axis=1)
    whole_span = jnp.sum(jnp.where(later[..., None], totals[None], 0.0), axis=1)
    ahead_weight = jnp.where(before_me[:, None], jnp.exp(ahead_span), 0.0)
    whole_weight = jnp.exp(whole_span)
    ahead = (
        jnp.sum(jnp.where(before_me[:, None], totals, 0.0), axis=0),
        jnp.sum(ahead_weight[:, :, None, None] * states.astype(f32), axis=0),
    )
    whole = (
        jnp.sum(totals, axis=0),
        jnp.sum(whole_weight[:, :, None, None] * states.astype(f32), axis=0),
    )
    return ahead, whole, rider


def device_prefix(total, state, levels, rider):
    value = (total, state)
    aheads = []
    answer = None
    for axes in levels:
        ahead, value, heard = level_scan(value, axes, rider)
        rider, answer = None, heard if rider is not None else answer
        aheads.append(ahead)
    entering = aheads[-1]
    for ahead in reversed(aheads[:-1]):
        entering = link(entering, ahead)
    return entering[1], answer


def attend_blocks(queries, own_keys, own_values, far_keys, far_values):
    score_scale = 1.0 / math.sqrt(P_SIZE)
    own_scores = (
        jnp.einsum("hbqd,hbkd->hbqk", queries, own_keys, preferred_element_type=f32) * score_scale
    )
    far_scores = (
        jnp.einsum("hbqd,hbkd->hbqk", queries, far_keys, preferred_element_type=f32) * score_scale
    )
    peak = jnp.maximum(
        jnp.max(own_scores, axis=-1, keepdims=True), jnp.max(far_scores, axis=-1, keepdims=True)
    )
    own_exp = jnp.exp(own_scores - peak)
    far_exp = jnp.exp(far_scores - peak)
    denominator = jnp.sum(own_exp, axis=-1, keepdims=True) + jnp.sum(
        far_exp, axis=-1, keepdims=True
    )
    own_weight = (own_exp / denominator).astype(bf16)
    far_weight = (far_exp / denominator).astype(bf16)
    mixed = jnp.einsum("hbqk,hbkd->hbqd", own_weight, own_values, preferred_element_type=f32)
    mixed = mixed + jnp.einsum(
        "hbqk,hbkd->hbqd", far_weight, far_values, preferred_element_type=f32
    )
    return mixed.astype(bf16)


def slot_ranks(owner_row, seq_count):
    owners_axis = jnp.arange(seq_count, dtype=jnp.int32)
    hits = (owner_row[:, None] == owners_axis[None, :]).astype(jnp.int32)
    return jnp.sum((jnp.cumsum(hits, axis=0) - hits) * hits, axis=1)


def per_device(
    tokens,
    norm_gain1,
    w_xz,
    w_bc,
    w_dt,
    dt_bias,
    decay_rate,
    curve_jump,
    skip_gain,
    norm_gain2,
    w_out,
    norm_gain3,
    w_q,
    w_kv,
    w_o,
    nbr_owner,
    nbr_block,
):
    token_count, width = tokens.shape
    seq_count = lax.axis_size(SEQ)
    block_count = token_count // BL
    request_count = block_count * KN
    slot_count = max(2, -(-request_count // seq_count))

    owner_flat = nbr_owner.reshape(-1)
    block_flat = nbr_block.reshape(-1)
    own_rank = slot_ranks(owner_flat, seq_count)
    targets = jnp.arange(seq_count, dtype=jnp.int32)[:, None, None]
    slots = jnp.arange(slot_count, dtype=jnp.int32)[None, :, None]
    match = (owner_flat[None, None, :] == targets) & (own_rank[None, None, :] == slots)
    wanted = jnp.sum(jnp.where(match, block_flat[None, None, :], 0), axis=2)
    arrival_index = owner_flat * slot_count + own_rank

    normed1 = rms_rows(tokens, norm_gain1)
    x = heads_of(normed1, w_xz[:, :INNER])
    z = heads_of(normed1, w_xz[:, INNER:])
    maps = jnp.dot(normed1, w_bc, preferred_element_type=f32).astype(bf16)
    dt = jnp.einsum("td,dh->ht", normed1, w_dt, preferred_element_type=f32)
    u = jax.nn.softplus(dt + dt_bias[:, None])
    log_decay = -(decay_rate[:, None] * u + curve_jump[None, :])
    y_intra, prefix, before, local_state, local_total, running, cc = chunk_parts(
        x, maps[:, :NS], maps[:, NS:], u, log_decay
    )
    entering, send_index = device_prefix(
        local_total, local_state, (("y", "c"), ("x",), ("z",)), wanted
    )
    chunk_in = jnp.exp(before)[:, :, None, None] * entering[:, None] + prefix
    arriving = jnp.einsum("ctn,hcpn->hctp", cc.astype(f32), chunk_in, precision=highest)
    ssm = (y_intra + jnp.exp(running)[..., None] * arriving).reshape(H, token_count, P_SIZE)

    total = ssm + skip_gain[:, None, None] * x.astype(f32)
    gated = total * jax.nn.silu(z.astype(f32))
    head_normed = gated * lax.rsqrt(jnp.mean(gated * gated, axis=-1, keepdims=True) + epsilon)
    scaled = (head_normed * norm_gain2.reshape(H, 1, P_SIZE)).astype(bf16)
    middle = (
        tokens.astype(f32)
        + jnp.einsum(
            "htp,hpd->td", scaled, w_out.reshape(H, P_SIZE, width), preferred_element_type=f32
        )
    ).astype(bf16)

    normed = rms_rows(middle, norm_gain3)
    own_rows = normed.reshape(block_count, BL, width)
    outgoing = own_rows[send_index]
    arrived = lax.all_to_all(outgoing, SEQ, split_axis=0, concat_axis=0, tiled=True)
    far_rows = arrived.reshape(seq_count * slot_count, BL, width)[arrival_index]
    far_rows = far_rows.reshape(request_count * BL, width)

    queries = heads_of(normed, w_q).reshape(H, block_count, BL, P_SIZE)
    own_keys = heads_of(normed, w_kv[:, :INNER]).reshape(H, block_count, BL, P_SIZE)
    own_values = heads_of(normed, w_kv[:, INNER:]).reshape(H, block_count, BL, P_SIZE)
    far_keys = heads_of(far_rows, w_kv[:, :INNER]).reshape(H, block_count, KN * BL, P_SIZE)
    far_values = heads_of(far_rows, w_kv[:, INNER:]).reshape(H, block_count, KN * BL, P_SIZE)
    attended = attend_blocks(queries, own_keys, own_values, far_keys, far_values)
    attended = attended.reshape(H, token_count, P_SIZE)
    return (
        middle.astype(f32)
        + jnp.einsum(
            "hte,hed->td", attended, w_o.reshape(H, P_SIZE, width), preferred_element_type=f32
        )
    ).astype(bf16)


def solution(mesh):
    seq_shape = (mesh.shape["grp"], 4, mesh.shape["seq"] // 8, 2)
    fine = jax.sharding.Mesh(mesh.devices.reshape(seq_shape), CURVE)
    rows = P(CURVE, None)
    whole = P()
    in_specs = (rows, whole, whole, whole, whole, whole, whole, P(CURVE)) + (whole,) * 7 + (rows, rows)
    return jax.shard_map(
        per_device, mesh=fine, in_specs=in_specs, out_specs=rows, check_vma=False
    )
```

```python
import math

import jax
import jax.numpy as jnp
from jax import lax
from jax.sharding import PartitionSpec as P

H = 16
P_SIZE = 64
NS = 128
INNER = 1024
CH = 128
BL = 64
KN = 2


epsilon = 1e-05
highest = lax.Precision.HIGHEST
f32 = jnp.float32
bf16 = jnp.bfloat16
SEQ = ("x", "y", "c")
CURVE = ("z", "x", "y", "c")
def rms_rows(values, weights):
    floats = values.astype(f32)
    return (
        floats * lax.rsqrt(jnp.mean(floats * floats, axis=-1, keepdims=True) + epsilon) * weights
    ).astype(bf16)


def heads_of(rows, weight):
    flat = jnp.dot(rows, weight, preferred_element_type=f32).astype(bf16)
    return flat.reshape(rows.shape[0], H, P_SIZE).transpose(1, 0, 2)


def chunk_parts(x, b, c, u, log_decay):
    count = x.shape[1] // CH
    xc = x.reshape(H, count, CH, P_SIZE)
    bc = b.reshape(count, CH, NS)
    cc = c.reshape(count, CH, NS)
    uc = u.reshape(H, count, CH)
    running = jnp.cumsum(log_decay.reshape(H, count, CH), axis=2)
    lower = (jnp.arange(CH)[:, None] >= jnp.arange(CH)[None, :])[None, None]
    spread = running[..., :, None] - running[..., None, :]
    weights = jnp.where(lower, jnp.exp(jnp.where(lower, spread, 0.0)), 0.0)
    intersection = jnp.einsum("ctn,csn->cts", cc, bc, preferred_element_type=f32)
    mixing = (intersection[None] * weights * uc[:, :, None, :]).astype(bf16)
    y_intra = jnp.einsum("hcts,hcsp->hctp", mixing, xc, preferred_element_type=f32)
    last = running[..., -1]
    tail_weight = jnp.exp(last[..., None] - running) * uc
    tail = (tail_weight[..., None] * xc.astype(f32)).astype(bf16)
    chunk_state = jnp.einsum("hcsp,csn->hcpn", tail, bc, preferred_element_type=f32)
    prefix = [jnp.zeros((H, P_SIZE, NS), f32)]
    before = [jnp.zeros((H,), f32)]
    for k in range(count):
        prefix.append(jnp.exp(last[:, k])[:, None, None] * prefix[-1] + chunk_state[:, k])
        before.append(before[-1] + last[:, k])
    return (
        y_intra,
        jnp.stack(prefix[:count], axis=1),
        jnp.stack(before[:count], axis=1),
        prefix[count],
        before[count],
        running,
        cc,
    )


def to_wire(total, state):
    high = total.astype(bf16)
    rest = total - high.astype(f32)
    middle = rest.astype(bf16)
    low = (rest - middle.astype(f32)).astype(bf16)
    pieces = jnp.pad(jnp.stack([high, middle, low]), ((0, 5), (0, NS - H)))
    return jnp.concatenate([state.reshape(H * P_SIZE, NS).astype(bf16), pieces], axis=0)


def from_wire(wire):
    pieces = wire[H * P_SIZE : H * P_SIZE + 3, :H].astype(f32)
    total = pieces[0] + pieces[1] + pieces[2]
    return total, wire[: H * P_SIZE].astype(f32).reshape(H, P_SIZE, NS)


def link(earlier, later):
    return (earlier[0] + later[0], jnp.exp(later[0])[:, None, None] * earlier[1] + later[1])


def level_scan(value, axes):
    members = lax.axis_size(axes)
    place = lax.axis_index(axes)
    wire = to_wire(*value)
    copies = jnp.broadcast_to(wire[None], (members,) + wire.shape)
    everyone = lax.all_to_all(copies, axes, split_axis=0, concat_axis=0, tiled=True)
    totals = jnp.sum(everyone[:, H * P_SIZE : H * P_SIZE + 3, :H].astype(f32), axis=1)
    states = everyone[:, : H * P_SIZE].reshape(members, H, P_SIZE, NS)
    order = jnp.arange(members)
    later = order[None, :] > order[:, None]
    before_me = order < place
    ahead_span = jnp.sum(jnp.where((later & before_me[None, :])[..., None], totals[None], 0.0), axis=1)
    whole_span = jnp.sum(jnp.where(later[..., None], totals[None], 0.0), axis=1)
    ahead_weight = jnp.where(before_me[:, None], jnp.exp(ahead_span), 0.0)
    whole_weight = jnp.exp(whole_span)
    ahead = (
        jnp.sum(jnp.where(before_me[:, None], totals, 0.0), axis=0),
        jnp.sum(ahead_weight[:, :, None, None] * states.astype(f32), axis=0),
    )
    whole = (
        jnp.sum(totals, axis=0),
        jnp.sum(whole_weight[:, :, None, None] * states.astype(f32), axis=0),
    )
    return ahead, whole


def device_prefix(total, state, levels):
    value = (total, state)
    aheads = []
    for axes in levels:
        ahead, value = level_scan(value, axes)
        aheads.append(ahead)
    entering = aheads[-1]
    for ahead in reversed(aheads[:-1]):
        entering = link(entering, ahead)
    return entering[1]


def attend_blocks(queries, own_keys, own_values, far_keys, far_values):
    score_scale = 1.0 / math.sqrt(P_SIZE)
    own_scores = (
        jnp.einsum("hbqd,hbkd->hbqk", queries, own_keys, preferred_element_type=f32) * score_scale
    )
    own_peak = jnp.max(own_scores, axis=-1, keepdims=True)
    own_exp = jnp.exp(own_scores - own_peak)
    own_sum = jnp.sum(own_exp, axis=-1, keepdims=True)
    own_mixed = jnp.einsum(
        "hbqk,hbkd->hbqd", own_exp.astype(bf16), own_values, preferred_element_type=f32
    )
    far_scores = (
        jnp.einsum("hbqd,hbkd->hbqk", queries, far_keys, preferred_element_type=f32) * score_scale
    )
    peak = jnp.maximum(own_peak, jnp.max(far_scores, axis=-1, keepdims=True))
    own_scale = jnp.exp(own_peak - peak)
    far_exp = jnp.exp(far_scores - peak)
    denominator = own_sum * own_scale + jnp.sum(far_exp, axis=-1, keepdims=True)
    far_mixed = jnp.einsum(
        "hbqk,hbkd->hbqd", far_exp.astype(bf16), far_values, preferred_element_type=f32
    )
    return ((own_mixed * own_scale + far_mixed) / denominator).astype(bf16)


def slot_ranks(owner_row, seq_count):
    owners_axis = jnp.arange(seq_count, dtype=jnp.int32)
    hits = (owner_row[:, None] == owners_axis[None, :]).astype(jnp.int32)
    return jnp.sum((jnp.cumsum(hits, axis=0) - hits) * hits, axis=1)


def per_device(
    tokens,
    norm_gain1,
    w_xz,
    w_bc,
    w_dt,
    dt_bias,
    decay_rate,
    curve_jump,
    skip_gain,
    norm_gain2,
    w_out,
    norm_gain3,
    w_q,
    w_kv,
    w_o,
    nbr_owner,
    nbr_block,
):
    token_count, width = tokens.shape
    seq_count = lax.axis_size(SEQ)
    block_count = token_count // BL
    request_count = block_count * KN
    slot_count = max(2, -(-request_count // seq_count))

    owner_flat = nbr_owner.reshape(-1)
    block_flat = nbr_block.reshape(-1)
    own_rank = slot_ranks(owner_flat, seq_count)
    targets = jnp.arange(seq_count, dtype=jnp.int32)[:, None, None]
    slots = jnp.arange(slot_count, dtype=jnp.int32)[None, :, None]
    match = (owner_flat[None, None, :] == targets) & (own_rank[None, None, :] == slots)
    wanted = jnp.sum(jnp.where(match, block_flat[None, None, :], 0), axis=2)
    send_index = lax.all_to_all(wanted, SEQ, split_axis=0, concat_axis=0, tiled=True)
    arrival_index = owner_flat * slot_count + own_rank

    normed1 = rms_rows(tokens, norm_gain1)
    x = heads_of(normed1, w_xz[:, :INNER])
    z = heads_of(normed1, w_xz[:, INNER:])
    maps = jnp.dot(normed1, w_bc, preferred_element_type=f32).astype(bf16)
    dt = jnp.einsum("td,dh->ht", normed1, w_dt, preferred_element_type=f32)
    u = jax.nn.softplus(dt + dt_bias[:, None])
    log_decay = -(decay_rate[:, None] * u + curve_jump[None, :])
    y_intra, prefix, before, local_state, local_total, running, cc = chunk_parts(
        x, maps[:, :NS], maps[:, NS:], u, log_decay
    )
    entering = device_prefix(local_total, local_state, (("y", "c"), ("x",), ("z",)))
    chunk_in = jnp.exp(before)[:, :, None, None] * entering[:, None] + prefix
    arriving = jnp.einsum("ctn,hcpn->hctp", cc.astype(f32), chunk_in, precision=highest)
    ssm = (y_intra + jnp.exp(running)[..., None] * arriving).reshape(H, token_count, P_SIZE)

    total = ssm + skip_gain[:, None, None] * x.astype(f32)
    gated = total * jax.nn.silu(z.astype(f32))
    head_normed = gated * lax.rsqrt(jnp.mean(gated * gated, axis=-1, keepdims=True) + epsilon)
    scaled = (head_normed * norm_gain2.reshape(H, 1, P_SIZE)).astype(bf16)
    middle = (
        tokens.astype(f32)
        + jnp.einsum(
            "htp,hpd->td", scaled, w_out.reshape(H, P_SIZE, width), preferred_element_type=f32
        )
    ).astype(bf16)

    normed = rms_rows(middle, norm_gain3)
    own_rows = normed.reshape(block_count, BL, width)
    outgoing = own_rows[send_index]
    arrived = lax.all_to_all(outgoing, SEQ, split_axis=0, concat_axis=0, tiled=True)
    far_rows = arrived.reshape(seq_count * slot_count, BL, width)[arrival_index]
    far_rows = far_rows.reshape(request_count * BL, width)

    queries = heads_of(normed, w_q).reshape(H, block_count, BL, P_SIZE)
    own_keys = heads_of(normed, w_kv[:, :INNER]).reshape(H, block_count, BL, P_SIZE)
    own_values = heads_of(normed, w_kv[:, INNER:]).reshape(H, block_count, BL, P_SIZE)
    far_keys = heads_of(far_rows, w_kv[:, :INNER]).reshape(H, block_count, KN * BL, P_SIZE)
    far_values = heads_of(far_rows, w_kv[:, INNER:]).reshape(H, block_count, KN * BL, P_SIZE)
    attended = attend_blocks(queries, own_keys, own_values, far_keys, far_values)
    attended = attended.reshape(H, token_count, P_SIZE)
    return (
        middle.astype(f32)
        + jnp.einsum(
            "hte,hed->td", attended, w_o.reshape(H, P_SIZE, width), preferred_element_type=f32
        )
    ).astype(bf16)


def solution(mesh):
    seq_shape = (mesh.shape["grp"], 4, mesh.shape["seq"] // 8, 2)
    fine = jax.sharding.Mesh(mesh.devices.reshape(seq_shape), CURVE)
    rows = P(CURVE, None)
    whole = P()
    in_specs = (rows, whole, whole, whole, whole, whole, whole, P(CURVE)) + (whole,) * 7 + (rows, rows)
    return jax.shard_map(
        per_device, mesh=fine, in_specs=in_specs, out_specs=rows, check_vma=False
    )
```

```python
import math

import jax
import jax.numpy as jnp
from jax import lax
from jax.sharding import PartitionSpec as P

H = 16
P_SIZE = 64
NS = 128
INNER = 1024
CH = 128
BL = 64
KN = 2


epsilon = 1e-05
highest = lax.Precision.HIGHEST
f32 = jnp.float32
bf16 = jnp.bfloat16
SEQ = ("x", "y", "c")
CURVE = ("z", "x", "y", "c")
def rms_rows(values, weights):
    floats = values.astype(f32)
    return (
        floats * lax.rsqrt(jnp.mean(floats * floats, axis=-1, keepdims=True) + epsilon) * weights
    ).astype(bf16)


def heads_of(rows, weight):
    flat = jnp.dot(rows, weight, preferred_element_type=f32).astype(bf16)
    return flat.reshape(rows.shape[0], H, P_SIZE).transpose(1, 0, 2)


def chunk_parts(x, b, c, u, log_decay):
    count = x.shape[1] // CH
    xc = x.reshape(H, count, CH, P_SIZE)
    bc = b.reshape(count, CH, NS)
    cc = c.reshape(count, CH, NS)
    uc = u.reshape(H, count, CH)
    running = jnp.cumsum(log_decay.reshape(H, count, CH), axis=2)
    lower = (jnp.arange(CH)[:, None] >= jnp.arange(CH)[None, :])[None, None]
    spread = running[..., :, None] - running[..., None, :]
    weights = jnp.where(lower, jnp.exp(jnp.where(lower, spread, 0.0)), 0.0)
    intersection = jnp.einsum("ctn,csn->cts", cc, bc, preferred_element_type=f32)
    mixing = (intersection[None] * weights * uc[:, :, None, :]).astype(bf16)
    y_intra = jnp.einsum("hcts,hcsp->hctp", mixing, xc, preferred_element_type=f32)
    last = running[..., -1]
    tail_weight = jnp.exp(last[..., None] - running) * uc
    tail = (tail_weight[..., None] * xc.astype(f32)).astype(bf16)
    chunk_state = jnp.einsum("hcsp,csn->hcpn", tail, bc, preferred_element_type=f32)
    prefix = [jnp.zeros((H, P_SIZE, NS), f32)]
    before = [jnp.zeros((H,), f32)]
    for k in range(count):
        prefix.append(jnp.exp(last[:, k])[:, None, None] * prefix[-1] + chunk_state[:, k])
        before.append(before[-1] + last[:, k])
    return (
        y_intra,
        jnp.stack(prefix[:count], axis=1),
        jnp.stack(before[:count], axis=1),
        prefix[count],
        before[count],
        running,
        cc,
    )


def to_wire(total, state):
    high = total.astype(bf16)
    rest = total - high.astype(f32)
    middle = rest.astype(bf16)
    low = (rest - middle.astype(f32)).astype(bf16)
    pieces = jnp.pad(jnp.stack([high, middle, low]), ((0, 5), (0, NS - H)))
    return jnp.concatenate([state.reshape(H * P_SIZE, NS).astype(bf16), pieces], axis=0)


def from_wire(wire):
    pieces = wire[H * P_SIZE : H * P_SIZE + 3, :H].astype(f32)
    total = pieces[0] + pieces[1] + pieces[2]
    return total, wire[: H * P_SIZE].astype(f32).reshape(H, P_SIZE, NS)


def link(earlier, later):
    return (earlier[0] + later[0], jnp.exp(later[0])[:, None, None] * earlier[1] + later[1])


def level_scan(value, axes):
    members = lax.axis_size(axes)
    place = lax.axis_index(axes)
    wire = to_wire(*value)
    copies = jnp.broadcast_to(wire[None], (members,) + wire.shape)
    everyone = lax.all_to_all(copies, axes, split_axis=0, concat_axis=0, tiled=True)
    totals = jnp.sum(everyone[:, H * P_SIZE : H * P_SIZE + 3, :H].astype(f32), axis=1)
    states = everyone[:, : H * P_SIZE].reshape(members, H, P_SIZE, NS)
    order = jnp.arange(members)
    later = order[None, :] > order[:, None]
    before_me = order < place
    ahead_span = jnp.sum(jnp.where((later & before_me[None, :])[..., None], totals[None], 0.0), axis=1)
    whole_span = jnp.sum(jnp.where(later[..., None], totals[None], 0.0), axis=1)
    ahead_weight = jnp.where(before_me[:, None], jnp.exp(ahead_span), 0.0)
    whole_weight = jnp.exp(whole_span)
    ahead = (
        jnp.sum(jnp.where(before_me[:, None], totals, 0.0), axis=0),
        jnp.sum(ahead_weight[:, :, None, None] * states.astype(f32), axis=0),
    )
    whole = (
        jnp.sum(totals, axis=0),
        jnp.sum(whole_weight[:, :, None, None] * states.astype(f32), axis=0),
    )
    return ahead, whole


def device_prefix(total, state, levels):
    value = (total, state)
    aheads = []
    for axes in levels:
        ahead, value = level_scan(value, axes)
        aheads.append(ahead)
    entering = aheads[-1]
    for ahead in reversed(aheads[:-1]):
        entering = link(entering, ahead)
    return entering[1]


def attend_blocks(queries, own_keys, own_values, far_keys, far_values):
    score_scale = 1.0 / math.sqrt(P_SIZE)
    own_scores = (
        jnp.einsum("hbqd,hbkd->hbqk", queries, own_keys, preferred_element_type=f32) * score_scale
    )
    own_peak = jnp.max(own_scores, axis=-1, keepdims=True)
    own_exp = jnp.exp(own_scores - own_peak)
    own_sum = jnp.sum(own_exp, axis=-1, keepdims=True)
    own_mixed = jnp.einsum(
        "hbqk,hbkd->hbqd", own_exp.astype(bf16), own_values, preferred_element_type=f32
    )
    far_scores = (
        jnp.einsum("hbqd,hbkd->hbqk", queries, far_keys, preferred_element_type=f32) * score_scale
    )
    peak = jnp.maximum(own_peak, jnp.max(far_scores, axis=-1, keepdims=True))
    own_scale = jnp.exp(own_peak - peak)
    far_exp = jnp.exp(far_scores - peak)
    denominator = own_sum * own_scale + jnp.sum(far_exp, axis=-1, keepdims=True)
    far_mixed = jnp.einsum(
        "hbqk,hbkd->hbqd", far_exp.astype(bf16), far_values, preferred_element_type=f32
    )
    return ((own_mixed * own_scale + far_mixed) * (1.0 / denominator)).astype(bf16)


def slot_ranks(owner_row, seq_count):
    owners_axis = jnp.arange(seq_count, dtype=jnp.int32)
    hits = (owner_row[:, None] == owners_axis[None, :]).astype(jnp.int32)
    return jnp.sum((jnp.cumsum(hits, axis=0) - hits) * hits, axis=1)


def per_device(
    tokens,
    norm_gain1,
    w_xz,
    w_bc,
    w_dt,
    dt_bias,
    decay_rate,
    curve_jump,
    skip_gain,
    norm_gain2,
    w_out,
    norm_gain3,
    w_q,
    w_kv,
    w_o,
    nbr_owner,
    nbr_block,
):
    token_count, width = tokens.shape
    seq_count = lax.axis_size(SEQ)
    block_count = token_count // BL
    request_count = block_count * KN
    slot_count = max(2, -(-request_count // seq_count))

    owner_flat = nbr_owner.reshape(-1)
    block_flat = nbr_block.reshape(-1)
    own_rank = slot_ranks(owner_flat, seq_count)
    targets = jnp.arange(seq_count, dtype=jnp.int32)[:, None, None]
    slots = jnp.arange(slot_count, dtype=jnp.int32)[None, :, None]
    match = (owner_flat[None, None, :] == targets) & (own_rank[None, None, :] == slots)
    wanted = jnp.sum(jnp.where(match, block_flat[None, None, :], 0), axis=2)
    send_index = lax.all_to_all(wanted, SEQ, split_axis=0, concat_axis=0, tiled=True)
    arrival_index = owner_flat * slot_count + own_rank

    normed1 = rms_rows(tokens, norm_gain1)
    x = heads_of(normed1, w_xz[:, :INNER])
    z = heads_of(normed1, w_xz[:, INNER:])
    maps = jnp.dot(normed1, w_bc, preferred_element_type=f32).astype(bf16)
    dt = jnp.einsum("td,dh->ht", normed1, w_dt, preferred_element_type=f32)
    u = jax.nn.softplus(dt + dt_bias[:, None])
    log_decay = -(decay_rate[:, None] * u + curve_jump[None, :])
    y_intra, prefix, before, local_state, local_total, running, cc = chunk_parts(
        x, maps[:, :NS], maps[:, NS:], u, log_decay
    )
    entering = device_prefix(local_total, local_state, (("y", "c"), ("x",), ("z",)))
    chunk_in = jnp.exp(before)[:, :, None, None] * entering[:, None] + prefix
    arriving = jnp.einsum("ctn,hcpn->hctp", cc.astype(f32), chunk_in, precision=highest)
    ssm = (y_intra + jnp.exp(running)[..., None] * arriving).reshape(H, token_count, P_SIZE)

    total = ssm + skip_gain[:, None, None] * x.astype(f32)
    gated = total * jax.nn.silu(z.astype(f32))
    head_normed = gated * lax.rsqrt(jnp.mean(gated * gated, axis=-1, keepdims=True) + epsilon)
    scaled = (head_normed * norm_gain2.reshape(H, 1, P_SIZE)).astype(bf16)
    middle = (
        tokens.astype(f32)
        + jnp.einsum(
            "htp,hpd->td", scaled, w_out.reshape(H, P_SIZE, width), preferred_element_type=f32
        )
    ).astype(bf16)

    normed = rms_rows(middle, norm_gain3)
    own_rows = normed.reshape(block_count, BL, width)
    outgoing = own_rows[send_index]
    arrived = lax.all_to_all(outgoing, SEQ, split_axis=0, concat_axis=0, tiled=True)
    far_rows = arrived.reshape(seq_count * slot_count, BL, width)[arrival_index]
    far_rows = far_rows.reshape(request_count * BL, width)

    queries = heads_of(normed, w_q).reshape(H, block_count, BL, P_SIZE)
    own_keys = heads_of(normed, w_kv[:, :INNER]).reshape(H, block_count, BL, P_SIZE)
    own_values = heads_of(normed, w_kv[:, INNER:]).reshape(H, block_count, BL, P_SIZE)
    far_keys = heads_of(far_rows, w_kv[:, :INNER]).reshape(H, block_count, KN * BL, P_SIZE)
    far_values = heads_of(far_rows, w_kv[:, INNER:]).reshape(H, block_count, KN * BL, P_SIZE)
    attended = attend_blocks(queries, own_keys, own_values, far_keys, far_values)
    attended = attended.reshape(H, token_count, P_SIZE)
    return (
        middle.astype(f32)
        + jnp.einsum(
            "hte,hed->td", attended, w_o.reshape(H, P_SIZE, width), preferred_element_type=f32
        )
    ).astype(bf16)


def solution(mesh):
    seq_shape = (mesh.shape["grp"], 4, mesh.shape["seq"] // 8, 2)
    fine = jax.sharding.Mesh(mesh.devices.reshape(seq_shape), CURVE)
    rows = P(CURVE, None)
    whole = P()
    in_specs = (rows, whole, whole, whole, whole, whole, whole, P(CURVE)) + (whole,) * 7 + (rows, rows)
    return jax.shard_map(
        per_device, mesh=fine, in_specs=in_specs, out_specs=rows, check_vma=False
    )
```
